512 devices in a mesh: ctx: 32 (over z, x), tp: 16 (over y, core).
Axes of the slice: x: 4, y: 8, z: 8, core: 2. Of those that a mesh axis runs over, the one named last changes fastest.
Arguments:
- hidden: bfloat16 [8192, 2048], P(('ctx', 'tp')), may hold values from -14 to 14
- in_weight: bfloat16 [2048, 2, 4096], P(None, None, 'tp'), may hold values from -0.125 to 0.125
- step_weight: bfloat16 [2048, 64], P(None, 'tp'), may hold values from -0.125 to 0.125
- group_weight: bfloat16 [256, 4, 2048], P('tp'), may hold values from -0.125 to 0.125
- conv_inner: float32 [4, 4096], P(None, 'tp'), may hold values from -3 to 3
- inner_bias: float32 [4096], P('tp'), may hold values from -2.5 to 2.5
- conv_group: float32 [4, 1024], replicated, may hold values from -3 to 3
- group_bias: float32 [1024], replicated, may hold values from -2.5 to 2.5
- step_bias: float32 [64], P('tp'), may hold values from -9.5 to 0
- log_rate: float32 [64], P('tp'), may hold values from -2.5 to -0.5
- skip_weight: float32 [64], P('tp'), may hold values from 0.25 to 1
- norm_gain: float32 [4096], P('tp'), may hold values from 0.1 to 1.9
- out_weight: bfloat16 [4096, 2048], P('tp'), may hold values from -0.09375 to 0.09375
Outputs:
- mixed: bfloat16 [8192, 2048], P(('ctx', 'tp'))
The draws below stay inside these ranges and needn't reach their ends.
All inputs are finite; a program needn't handle non-finite values.
Results may differ from the reference program's by a relative error of at most 0.024.
Values may be sent and summed in bfloat16 or wider, within the bound.
No kernel may reach another device: no remote copies, remote signals or barrier semaphores. Data moves between devices by JAX's collectives and lax.ppermute only.
A program may use at most 64 MiB of HBM per device.

```python
import jax
import jax.numpy as jnp
from jax import lax

D = 2048
HEADS = 64
HEAD_DIM = 64
STATE = 128
GROUPS = 4
BLOCK = 256
KERNEL = 4
SEQUENCE_LENGTH = 8192
INNER = 4096


def draw_hidden(key, part):
    root_random_key = jax.random.fold_in(key, 0)
    segment_random_key = jax.random.fold_in(key, 2)
    value_entries = jax.random.truncated_normal(root_random_key, -2.0, 2.0, (SEQUENCE_LENGTH, D), jnp.float32)
    segment_runs = jax.random.uniform(segment_random_key, (SEQUENCE_LENGTH, 1), jnp.float32) < 1.0 / 1024
    return jnp.where(segment_runs, 4.0 * value_entries, value_entries).astype(jnp.bfloat16)


def draw_step_bias(key, part):
    pick_key, slow_key, fast_key = jax.random.split(key, 3)
    fraction = 0.5
    chooser = jax.random.uniform(pick_key, (HEADS,), jnp.float32)
    slow_value = jax.random.uniform(slow_key, (HEADS,), jnp.float32, -9.5, -8.5)
    fast_value = jax.random.uniform(fast_key, (HEADS,), jnp.float32, -2.0, 0.0)
    return jnp.where(chooser < fraction, slow_value, fast_value)


def steps_of(key, dims, pieces, smallest, top_value):
    def one(dim, parts):
        draws = jax.random.uniform(jax.random.fold_in(jax.random.fold_in(key, 6), dim), (parts,), jnp.float32, smallest / len(pieces), top_value / len(pieces))
        return jnp.repeat(jnp.exp(draws), dims[dim] // parts).reshape((-1,) + (1,) * (len(dims) - dim - 1))

    gain = one(*pieces[0])
    for cut in pieces[1:]:
        gain = gain * one(*cut)
    return gain


def centred(own_key, dims, width, reach, shards=(), held_as=jnp.bfloat16):
    entries = jax.random.normal(own_key, dims, jnp.float32) * width
    if len(shards) > 0:
        entries = steps_of(own_key, dims, shards, -0.22, 0.18) * entries
    return jnp.clip(entries, min=-reach, max=reach).astype(held_as)


def setup_inputs(seed: int = 0) -> dict:
    arg_keys = jax.random.split(jax.random.key(seed), 14)
    return {
        "hidden": draw_hidden(jax.random.fold_in(arg_keys[13], 71), 0),
        "in_weight": centred(arg_keys[1], (D, 2, INNER), D ** -0.5, 0.125, ((2, 16),)),
        "step_weight": centred(arg_keys[2], (D, HEADS), D ** -0.5, 0.125, ((1, 16),)),
        "group_weight": centred(arg_keys[3], (2 * STATE, GROUPS, D), D ** -0.5, 0.125, ((0, 16),)),
        "conv_inner": centred(arg_keys[4], (KERNEL, INNER), KERNEL ** -0.5, 3.0, ((1, 16),), jnp.float32),
        "inner_bias": centred(arg_keys[5], (INNER,), 0.5, 2.5, ((0, 16),), jnp.float32),
        "conv_group": centred(arg_keys[6], (KERNEL, 2 * GROUPS * STATE), KERNEL ** -0.5, 3.0, (), jnp.float32),
        "group_bias": centred(arg_keys[7], (2 * GROUPS * STATE,), 0.5, 2.5, (), jnp.float32),
        "step_bias": draw_step_bias(jax.random.fold_in(arg_keys[13], 71), 0),
        "log_rate": jnp.clip(-2.5 + 2.0 * jax.random.uniform(arg_keys[9], (HEADS,), jnp.float32) ** steps_of(arg_keys[9], (HEADS,), ((0, 16),), -0.2, 0.2), -2.5, -0.5),
        "skip_weight": jnp.clip(0.25 + 0.75 * jax.random.uniform(arg_keys[10], (HEADS,), jnp.float32) ** steps_of(arg_keys[10], (HEADS,), ((0, 16),), -0.2, 0.2), 0.25, 1.0),
        "norm_gain": jnp.clip(1.0 + 0.18 * jax.random.normal(arg_keys[11], (INNER,), jnp.float32), 0.1, 1.9),
        "out_weight": centred(arg_keys[12], (INNER, D), INNER ** -0.5, 0.09375, ((0, 16),)),
    }


def causal_conv(prior_rows, raw_rows, conv_weight, conv_bias):
    joined = jnp.concatenate([prior_rows, raw_rows], axis=0).astype(jnp.float32)
    length = raw_rows.shape[0]
    running = jnp.broadcast_to(conv_bias.astype(jnp.float32)[None, :], raw_rows.shape)
    for offset in range(conv_weight.shape[0]):
        running = running + conv_weight[offset][None, :] * joined[offset:offset + length]
    return jax.nn.silu(running).astype(jnp.bfloat16)

def reference(hidden, in_weight, step_weight, group_weight, conv_inner, inner_bias, conv_group, group_bias, step_bias, log_rate, skip_weight, norm_gain, out_weight):
    highest = lax.Precision.HIGHEST
    zx_rows = jnp.dot(hidden, in_weight.reshape(D, 2 * INNER), preferred_element_type=jnp.float32).astype(jnp.bfloat16)
    gate_raw = zx_rows[:, :INNER]
    inner_raw = zx_rows[:, INNER:]
    group_matrix = jnp.transpose(group_weight, (1, 0, 2)).reshape(GROUPS * 2 * STATE, D)
    map_raw = lax.dot_general(hidden, group_matrix, (((1,), (1,)), ((), ())), preferred_element_type=jnp.float32).astype(jnp.bfloat16)
    step_raw = jnp.dot(hidden, step_weight, preferred_element_type=jnp.float32).astype(jnp.bfloat16)
    x_conv = causal_conv(jnp.zeros((KERNEL - 1, INNER), jnp.bfloat16), inner_raw, conv_inner, inner_bias)
    maps = causal_conv(jnp.zeros((KERNEL - 1, 2 * GROUPS * STATE), jnp.bfloat16), map_raw, conv_group, group_bias)
    maps = maps.reshape(SEQUENCE_LENGTH, GROUPS, 2, STATE)
    step_size = jax.nn.softplus(step_raw.astype(jnp.float32) + step_bias[None, :])
    decay_rate = -jnp.exp(log_rate)
    blocks = SEQUENCE_LENGTH // BLOCK
    per_group = HEADS // GROUPS
    x_blocks = x_conv.reshape(blocks, BLOCK, HEADS, HEAD_DIM)
    input_map = maps[:, :, 0, :].reshape(blocks, BLOCK, GROUPS, STATE)
    output_map = maps[:, :, 1, :].reshape(blocks, BLOCK, GROUPS, STATE)
    step_blocks = step_size.reshape(blocks, BLOCK, HEADS)
    causal = jnp.arange(BLOCK)[:, None] >= jnp.arange(BLOCK)[None, :]

    def block_step(carry, item):
        x_vals, in_map, out_map, steps_here = item
        log_step = (steps_here * decay_rate[None, :]).T
        cumulative = jnp.cumsum(log_step, axis=1)
        scores = jnp.einsum('ign,jgn->gij', out_map.astype(jnp.float32), in_map.astype(jnp.float32), precision=highest)
        scores = jnp.repeat(scores, per_group, axis=0)
        exponent = jnp.where(causal[None], cumulative[:, :, None] - cumulative[:, None, :], -jnp.inf)
        mixing = (scores * jnp.exp(exponent) * steps_here.T[:, None, :]).astype(jnp.bfloat16)
        mixing = lax.optimization_barrier(mixing).astype(jnp.float32)
        x_float = x_vals.astype(jnp.float32)
        within = jnp.einsum('hij,jhp->ihp', mixing, x_float, precision=highest)
        out_heads = jnp.repeat(out_map, per_group, axis=1).astype(jnp.float32)
        in_heads = jnp.repeat(in_map, per_group, axis=1).astype(jnp.float32)
        start_low = lax.optimization_barrier(carry.astype(jnp.bfloat16)).astype(jnp.float32)
        carried = jnp.exp(cumulative).T[:, :, None] * jnp.einsum('ihn,hpn->ihp', out_heads, start_low, precision=highest)
        weight = jnp.exp(cumulative[:, -1:] - cumulative) * steps_here.T
        weighted = (x_float * weight.T[:, :, None]).astype(jnp.bfloat16)
        weighted = lax.optimization_barrier(weighted).astype(jnp.float32)
        block_state = jnp.einsum('jhp,jhn->hpn', weighted, in_heads, precision=highest)
        result_heads = within + carried + skip_weight[None, :, None] * x_float
        following = jnp.exp(cumulative[:, -1])[:, None, None] * carry + block_state
        return (following, result_heads)
    initial = jnp.zeros((HEADS, HEAD_DIM, STATE), jnp.float32)
    final_state, result_blocks = lax.scan(block_step, initial, (x_blocks, input_map, output_map, step_blocks))
    result_heads = result_blocks.reshape(SEQUENCE_LENGTH, INNER)
    gated = result_heads * jax.nn.silu(gate_raw.astype(jnp.float32))
    grouped = gated.reshape(SEQUENCE_LENGTH, GROUPS, INNER // GROUPS)
    inverse = lax.rsqrt(lax.optimization_barrier(jnp.mean(grouped * grouped, axis=2)) + 1e-05)
    normed = ((grouped * inverse[:, :, None]).reshape(SEQUENCE_LENGTH, INNER) * norm_gain[None, :]).astype(jnp.bfloat16)
    return jnp.dot(normed, out_weight, preferred_element_type=jnp.float32).astype(jnp.bfloat16)
```

```python
import jax
import jax.numpy as jnp
from jax import lax
from jax.sharding import PartitionSpec as P

HEADS = 64
HEAD_DIM = 64
STATE = 128
GROUPS = 4
BLOCK = 256
KERNEL = 4


def shifted(x, axis, by):
    peers = lax.axis_size(axis)
    pairs = [(i, i + by) for i in range(peers) if 0 <= i + by < peers]
    return lax.ppermute(x, axis, pairs)


def swapped(x, axis, bit):
    peers = lax.axis_size(axis)
    return lax.ppermute(x, axis, [(i, i ^ bit) for i in range(peers)])


def gather_rows(rows, axis, bits):
    place = lax.axis_index(axis)
    peers = lax.axis_size(axis)
    held = rows
    for bit in reversed(bits):
        other = swapped(held, axis, bit)
        low = (place & bit) == 0
        held = jnp.where(low, jnp.stack([held, other]), jnp.stack([other, held]))
    order = tuple(reversed(range(len(bits)))) + tuple(range(len(bits), held.ndim))
    held = jnp.transpose(held, order)
    return held.reshape((peers * rows.shape[0],) + rows.shape[1:])


def scatter_sum(full, axis, bits):
    place = lax.axis_index(axis)
    peers = lax.axis_size(axis)
    per = full.shape[0] // peers
    held = full.reshape((2,) * len(bits) + (per,) + full.shape[1:])
    for bit in bits:
        at = held.ndim - len(full.shape) - 1
        mine = (place // bit) % 2
        keep = lax.dynamic_index_in_dim(held, mine, at, keepdims=False)
        give = lax.dynamic_index_in_dim(held, 1 - mine, at, keepdims=False)
        held = keep + swapped(give, axis, bit)
    return held.reshape((per,) + full.shape[1:])


def causal_conv(prior_rows, raw_rows, conv_weight, conv_bias):
    joined = jnp.concatenate([prior_rows, raw_rows], axis=0).astype(jnp.float32)
    length = raw_rows.shape[0]
    running = jnp.broadcast_to(conv_bias[None, :], raw_rows.shape)
    for offset in range(conv_weight.shape[0]):
        running = running + conv_weight[offset][None, :] * joined[offset : offset + length]
    return jax.nn.silu(running).astype(jnp.bfloat16)


def body(
    hidden,
    in_weight,
    step_weight,
    group_weight,
    conv_inner,
    inner_bias,
    conv_group,
    group_bias,
    step_bias,
    log_rate,
    skip_weight,
    norm_gain,
    out_weight,
):
    tp_size = lax.axis_size("tp")
    tp_bits = [1 << k for k in range(tp_size.bit_length() - 1)]
    heads_dev = log_rate.shape[0]
    inner_dev = in_weight.shape[2]
    group_cols = 2 * STATE
    per_group_dev = (HEADS // GROUPS) // heads_dev
    group_index = lax.axis_index("tp") // per_group_dev
    zx_weight = in_weight.reshape(in_weight.shape[0], 2 * inner_dev)
    shard_rows = gather_rows(hidden, "tp", tp_bits)
    length = shard_rows.shape[0]
    projected = jnp.concatenate(
        [
            jnp.dot(shard_rows, zx_weight, preferred_element_type=jnp.float32),
            jnp.dot(shard_rows, step_weight, preferred_element_type=jnp.float32),
        ],
        axis=1,
    ).astype(jnp.bfloat16)
    gate_raw = projected[:, :inner_dev]
    inner_raw = projected[:, inner_dev : 2 * inner_dev]
    step_raw = projected[:, 2 * inner_dev :]
    dest_groups = [q // per_group_dev for q in range(tp_size)]
    spread = jnp.take(group_weight, jnp.array(dest_groups), axis=1)
    own_maps = jnp.einsum(
        "td,sqd->qts", shard_rows, spread, preferred_element_type=jnp.float32
    ).astype(jnp.bfloat16)
    got_maps = lax.all_to_all(own_maps, "tp", 0, 0, tiled=True)
    map_part = jnp.transpose(got_maps, (1, 0, 2)).reshape(length, group_cols)
    border_rows = KERNEL - 1
    prior = shifted(
        jnp.concatenate([inner_raw[length - border_rows :], map_part[length - border_rows :]], axis=1),
        "ctx",
        1,
    )
    inner_prior = prior[:, :inner_dev]
    map_prior = prior[:, inner_dev:]
    x_conv = causal_conv(inner_prior, inner_raw, conv_inner, inner_bias)
    own_taps = lax.dynamic_slice_in_dim(conv_group, group_index * group_cols, group_cols, 1)
    own_bias = lax.dynamic_slice_in_dim(group_bias, group_index * group_cols, group_cols, 0)
    maps = causal_conv(map_prior, map_part, own_taps, own_bias)
    step_size = jax.nn.softplus(step_raw.astype(jnp.float32) + step_bias[None, :])
    decay_rate = -jnp.exp(log_rate)
    blocks = length // BLOCK
    x_blocks = x_conv.reshape(blocks, BLOCK, heads_dev, HEAD_DIM)
    input_map = maps[:, :STATE].reshape(blocks, BLOCK, STATE)
    output_map = maps[:, STATE:].reshape(blocks, BLOCK, STATE)
    step_blocks = jnp.swapaxes(step_size.reshape(blocks, BLOCK, heads_dev), 1, 2)
    cumulative = jnp.cumsum(step_blocks * decay_rate[None, :, None], axis=2)
    scores = jnp.einsum("kin,kjn->kij", output_map, input_map, preferred_element_type=jnp.float32)
    causal = jnp.arange(BLOCK)[:, None] >= jnp.arange(BLOCK)[None, :]
    exponent = jnp.where(causal, cumulative[..., :, None] - cumulative[..., None, :], -jnp.inf)
    mixing = (scores[:, None] * jnp.exp(exponent) * step_blocks[..., None, :]).astype(jnp.bfloat16)
    within = jnp.einsum("khij,kjhp->kihp", mixing, x_blocks, preferred_element_type=jnp.float32)
    weight = jnp.exp(cumulative[..., BLOCK - 1 :] - cumulative) * step_blocks
    x_float = x_blocks.astype(jnp.float32)
    weighted = (x_float * jnp.swapaxes(weight, 1, 2)[..., None]).astype(jnp.bfloat16)
    block_state = jnp.einsum(
        "kjhp,kjn->khpn", weighted, input_map, preferred_element_type=jnp.float32
    )
    block_decay = jnp.exp(cumulative[..., BLOCK - 1])

    def advance(carry, item):
        running, product = carry
        block_stop_index, state_here = item
        return (
            (block_stop_index[:, None, None] * running + state_here, product * block_stop_index),
            (running, product),
        )

    empty_state = jnp.zeros((heads_dev, HEAD_DIM, STATE), jnp.float32)
    (dev_state, dev_decay), (local_starts, prefixes) = lax.scan(
        advance, (empty_state, jnp.ones((heads_dev,), jnp.float32)), (block_decay, block_state)
    )
    ctx_size = lax.axis_size("ctx")
    place = lax.axis_index("ctx")
    in_decay = jnp.ones_like(dev_decay)
    in_state = jnp.zeros_like(dev_state)
    run_decay = dev_decay
    run_state = dev_state
    reach = 1
    while reach < ctx_size:
        packed = jnp.concatenate(
            [run_state, jnp.broadcast_to(run_decay[:, None, None], (heads_dev, 1, STATE))], axis=1
        )
        got = shifted(packed, "ctx", reach)
        valid = place >= reach
        got_state = jnp.where(valid, got[:, :HEAD_DIM], 0.0)
        got_decay = jnp.where(valid, got[:, HEAD_DIM, 0], 1.0)
        in_state = in_decay[:, None, None] * got_state + in_state
        in_decay = got_decay * in_decay
        run_state = run_decay[:, None, None] * got_state + run_state
        run_decay = got_decay * run_decay
        reach *= 2
    incoming = in_state
    starting = local_starts + prefixes[:, :, None, None] * incoming[None]
    carried = jnp.einsum(
        "kin,khpn->kihp",
        output_map,
        starting.astype(jnp.bfloat16),
        preferred_element_type=jnp.float32,
    )
    carried = carried * jnp.swapaxes(jnp.exp(cumulative), 1, 2)[..., None]
    result_heads = within + carried + skip_weight[None, None, :, None] * x_float
    result_heads = result_heads.reshape(length, inner_dev)
    gated = result_heads * jax.nn.silu(gate_raw.astype(jnp.float32))
    total = jnp.sum(gated * gated, axis=1)
    bit = 1
    while bit < per_group_dev:
        total = total + swapped(total, "tp", bit)
        bit *= 2
    inverse = lax.rsqrt(total / (HEADS * HEAD_DIM // GROUPS) + 1e-05)
    normed = (gated * inverse[:, None] * norm_gain[None, :]).astype(jnp.bfloat16)
    mixed = scatter_sum(
        jnp.dot(normed, out_weight, preferred_element_type=jnp.float32), "tp", tp_bits
    )
    return mixed.astype(jnp.bfloat16)


def solution(mesh):
    placed = (
        P(("ctx", "tp"), None),
        P(None, None, "tp"),
        P(None, "tp"),
        P("tp", None, None),
        P(None, "tp"),
        P("tp"),
        P(),
        P(),
        P("tp"),
        P("tp"),
        P("tp"),
        P("tp"),
        P("tp", None),
    )
    return jax.shard_map(
        body, mesh=mesh, in_specs=placed, out_specs=P(("ctx", "tp"), None), check_vma=False
    )
```

```python
import jax
import jax.numpy as jnp
from jax import lax
from jax.sharding import PartitionSpec as P

HEADS = 64
HEAD_DIM = 64
STATE = 128
GROUPS = 4
BLOCK = 256
KERNEL = 4


def shifted(x, axis, by):
    peers = lax.axis_size(axis)
    pairs = [(i, i + by) for i in range(peers) if 0 <= i + by < peers]
    return lax.ppermute(x, axis, pairs)


def swapped(x, axis, bit):
    peers = lax.axis_size(axis)
    return lax.ppermute(x, axis, [(i, i ^ bit) for i in range(peers)])


def gather_rows(rows, axis, bits):
    place = lax.axis_index(axis)
    peers = lax.axis_size(axis)
    held = rows
    for bit in reversed(bits):
        other = swapped(held, axis, bit)
        low = (place & bit) == 0
        held = jnp.where(low, jnp.stack([held, other]), jnp.stack([other, held]))
    order = tuple(reversed(range(len(bits)))) + tuple(range(len(bits), held.ndim))
    held = jnp.transpose(held, order)
    return held.reshape((peers * rows.shape[0],) + rows.shape[1:])


def halve(full, axis, bits, levels):
    place = lax.axis_index(axis)
    held = full
    if full.ndim < levels + 2:
        held = full.reshape((2,) * levels + (full.shape[0] >> levels,) + full.shape[1:])
    for bit in bits:
        at = held.ndim - 3
        mine = (place // bit) % 2
        keep = lax.dynamic_index_in_dim(held, mine, at, keepdims=False)
        give = lax.dynamic_index_in_dim(held, 1 - mine, at, keepdims=False)
        held = keep + swapped(give.astype(jnp.bfloat16), axis, bit).astype(jnp.float32)
    return held


def causal_conv(prior_rows, raw_rows, conv_weight, conv_bias):
    joined = jnp.concatenate([prior_rows, raw_rows], axis=0).astype(jnp.float32)
    length = raw_rows.shape[0]
    running = jnp.broadcast_to(conv_bias[None, :], raw_rows.shape)
    for offset in range(conv_weight.shape[0]):
        running = running + conv_weight[offset][None, :] * joined[offset : offset + length]
    return jax.nn.silu(running).astype(jnp.bfloat16)


def body(
    hidden,
    in_weight,
    step_weight,
    group_weight,
    conv_inner,
    inner_bias,
    conv_group,
    group_bias,
    step_bias,
    log_rate,
    skip_weight,
    norm_gain,
    out_weight,
):
    tp_size = lax.axis_size("tp")
    tp_bits = [1 << k for k in range(tp_size.bit_length() - 1)]
    heads_dev = log_rate.shape[0]
    inner_dev = in_weight.shape[2]
    group_cols = 2 * STATE
    per_group_dev = (HEADS // GROUPS) // heads_dev
    group_index = lax.axis_index("tp") // per_group_dev
    zx_weight = in_weight.reshape(in_weight.shape[0], 2 * inner_dev)
    shard_rows = gather_rows(hidden, "tp", tp_bits)
    length = shard_rows.shape[0]
    projected = jnp.concatenate(
        [
            jnp.dot(shard_rows, zx_weight, preferred_element_type=jnp.float32),
            jnp.dot(shard_rows, step_weight, preferred_element_type=jnp.float32),
        ],
        axis=1,
    ).astype(jnp.bfloat16)
    gate_raw = projected[:, :inner_dev]
    inner_raw = projected[:, inner_dev : 2 * inner_dev]
    step_raw = projected[:, 2 * inner_dev :]
    dest_groups = [q // per_group_dev for q in range(tp_size)]
    spread = jnp.take(group_weight, jnp.array(dest_groups), axis=1)
    own_maps = jnp.einsum(
        "td,sqd->qts", shard_rows, spread, preferred_element_type=jnp.float32
    ).astype(jnp.bfloat16)
    got_maps = lax.all_to_all(own_maps, "tp", 0, 0, tiled=True)
    map_part = jnp.transpose(got_maps, (1, 0, 2)).reshape(length, group_cols)
    border_rows = KERNEL - 1
    prior = shifted(
        jnp.concatenate([inner_raw[length - border_rows :], map_part[length - border_rows :]], axis=1),
        "ctx",
        1,
    )
    inner_prior = prior[:, :inner_dev]
    map_prior = prior[:, inner_dev:]
    x_conv = causal_conv(inner_prior, inner_raw, conv_inner, inner_bias)
    own_taps = lax.dynamic_slice_in_dim(conv_group, group_index * group_cols, group_cols, 1)
    own_bias = lax.dynamic_slice_in_dim(group_bias, group_index * group_cols, group_cols, 0)
    maps = causal_conv(map_prior, map_part, own_taps, own_bias)
    step_size = jax.nn.softplus(step_raw.astype(jnp.float32) + step_bias[None, :])
    decay_rate = -jnp.exp(log_rate)
    blocks = length // BLOCK
    x_blocks = x_conv.reshape(blocks, BLOCK, heads_dev, HEAD_DIM)
    input_map = maps[:, :STATE].reshape(blocks, BLOCK, STATE)
    output_map = maps[:, STATE:].reshape(blocks, BLOCK, STATE)
    step_blocks = jnp.swapaxes(step_size.reshape(blocks, BLOCK, heads_dev), 1, 2)
    cumulative = jnp.cumsum(step_blocks * decay_rate[None, :, None], axis=2)
    scores = jnp.einsum("kin,kjn->kij", output_map, input_map, preferred_element_type=jnp.float32)
    causal = jnp.arange(BLOCK)[:, None] >= jnp.arange(BLOCK)[None, :]
    exponent = jnp.where(causal, cumulative[..., :, None] - cumulative[..., None, :], -jnp.inf)
    mixing = (scores[:, None] * jnp.exp(exponent) * step_blocks[..., None, :]).astype(jnp.bfloat16)
    within = jnp.einsum("khij,kjhp->kihp", mixing, x_blocks, preferred_element_type=jnp.float32)
    weight = jnp.exp(cumulative[..., BLOCK - 1 :] - cumulative) * step_blocks
    x_float = x_blocks.astype(jnp.float32)
    weighted = (x_float * jnp.swapaxes(weight, 1, 2)[..., None]).astype(jnp.bfloat16)
    block_state = jnp.einsum(
        "kjhp,kjn->khpn", weighted, input_map, preferred_element_type=jnp.float32
    )
    block_decay = jnp.exp(cumulative[..., BLOCK - 1])

    def advance(carry, item):
        running, product = carry
        block_stop_index, state_here = item
        return (
            (block_stop_index[:, None, None] * running + state_here, product * block_stop_index),
            (running, product),
        )

    empty_state = jnp.zeros((heads_dev, HEAD_DIM, STATE), jnp.float32)
    (dev_state, dev_decay), (local_starts, prefixes) = lax.scan(
        advance, (empty_state, jnp.ones((heads_dev,), jnp.float32)), (block_decay, block_state)
    )
    ctx_size = lax.axis_size("ctx")
    place = lax.axis_index("ctx")
    in_decay = jnp.ones_like(dev_decay)
    in_state = jnp.zeros_like(dev_state)
    run_decay = dev_decay
    run_state = dev_state
    reach = 1
    while reach < ctx_size:
        packed = jnp.concatenate(
            [run_state, jnp.broadcast_to(run_decay[:, None, None], (heads_dev, 1, STATE))], axis=1
        )
        got = shifted(packed, "ctx", reach)
        valid = place >= reach
        got_state = jnp.where(valid, got[:, :HEAD_DIM], 0.0)
        got_decay = jnp.where(valid, got[:, HEAD_DIM, 0], 1.0)
        in_state = in_decay[:, None, None] * got_state + in_state
        in_decay = got_decay * in_decay
        run_state = run_decay[:, None, None] * got_state + run_state
        run_decay = got_decay * run_decay
        reach *= 2
    incoming = in_state
    starting = local_starts + prefixes[:, :, None, None] * incoming[None]
    carried = jnp.einsum(
        "kin,khpn->kihp",
        output_map,
        starting.astype(jnp.bfloat16),
        preferred_element_type=jnp.float32,
    )
    carried = carried * jnp.swapaxes(jnp.exp(cumulative), 1, 2)[..., None]
    result_heads = within + carried + skip_weight[None, None, :, None] * x_float
    result_heads = result_heads.reshape(length, inner_dev)
    gated = result_heads * jax.nn.silu(gate_raw.astype(jnp.float32))
    squares = jnp.sum(gated * gated, axis=1)
    scaled = (gated * norm_gain[None, :]).astype(jnp.bfloat16)
    partial = jnp.dot(scaled, out_weight, preferred_element_type=jnp.float32)
    width = partial.shape[1]
    packed = jnp.concatenate([partial, jnp.broadcast_to(squares[:, None], (length, 128))], axis=1)
    within_bits = [bit for bit in tp_bits if bit < per_group_dev]
    across_bits = [bit for bit in tp_bits if bit >= per_group_dev]
    held = halve(packed, "tp", within_bits, len(tp_bits))
    inverse = lax.rsqrt(held[..., width] / (HEADS * HEAD_DIM // GROUPS) + 1e-05)
    held = held[..., :width] * inverse[..., None]
    held = halve(held, "tp", across_bits, len(across_bits))
    mixed = held.reshape(length // tp_size, width)
    return mixed.astype(jnp.bfloat16)


def solution(mesh):
    placed = (
        P(("ctx", "tp"), None),
        P(None, None, "tp"),
        P(None, "tp"),
        P("tp", None, None),
        P(None, "tp"),
        P("tp"),
        P(),
        P(),
        P("tp"),
        P("tp"),
        P("tp"),
        P("tp"),
        P("tp", None),
    )
    return jax.shard_map(
        body, mesh=mesh, in_specs=placed, out_specs=P(("ctx", "tp"), None), check_vma=False
    )
```

```python
import jax
import jax.numpy as jnp
from jax import lax
from jax.sharding import PartitionSpec as P

HEADS = 64
HEAD_DIM = 64
STATE = 128
GROUPS = 4
BLOCK = 256
KERNEL = 4


def shifted(x, axis, by):
    peers = lax.axis_size(axis)
    pairs = [(i, i + by) for i in range(peers) if 0 <= i + by < peers]
    return lax.ppermute(x, axis, pairs)


def swapped(x, axis, bit):
    peers = lax.axis_size(axis)
    return lax.ppermute(x, axis, [(i, i ^ bit) for i in range(peers)])


def gather_rows(rows, axis, bits):
    place = lax.axis_index(axis)
    peers = lax.axis_size(axis)
    held = rows
    for bit in reversed(bits):
        other = swapped(held, axis, bit)
        low = (place & bit) == 0
        held = jnp.where(low, jnp.stack([held, other]), jnp.stack([other, held]))
    return held


def halve(held, axis, bits):
    place = lax.axis_index(axis)
    for bit in bits:
        mine = (place // bit) % 2
        keep = lax.dynamic_index_in_dim(held, mine, 0, keepdims=False)
        give = lax.dynamic_index_in_dim(held, 1 - mine, 0, keepdims=False)
        held = keep + swapped(give.astype(jnp.bfloat16), axis, bit).astype(jnp.float32)
    return held


def causal_conv(prior_rows, raw_rows, conv_weight, conv_bias):
    joined = jnp.concatenate([prior_rows, raw_rows], axis=0).astype(jnp.float32)
    length = raw_rows.shape[0]
    running = jnp.broadcast_to(conv_bias[None, :], raw_rows.shape)
    for offset in range(conv_weight.shape[0]):
        running = running + conv_weight[offset][None, :] * joined[offset : offset + length]
    return jax.nn.silu(running).astype(jnp.bfloat16)


def body(
    hidden,
    in_weight,
    step_weight,
    group_weight,
    conv_inner,
    inner_bias,
    conv_group,
    group_bias,
    step_bias,
    log_rate,
    skip_weight,
    norm_gain,
    out_weight,
):
    tp_size = lax.axis_size("tp")
    tp_bits = [1 << k for k in range(tp_size.bit_length() - 1)]
    heads_dev = log_rate.shape[0]
    inner_dev = in_weight.shape[2]
    group_cols = 2 * STATE
    per_group_dev = (HEADS // GROUPS) // heads_dev
    group_index = lax.axis_index("tp") // per_group_dev
    zx_weight = in_weight.reshape(in_weight.shape[0], 2 * inner_dev)
    stacked = gather_rows(hidden, "tp", tp_bits)
    levels = len(tp_bits)
    length = tp_size * hidden.shape[0]
    flipped = tuple(reversed(range(levels)))

    def in_order(rows):
        rows = jnp.transpose(rows, flipped + tuple(range(levels, rows.ndim)))
        return rows.reshape((length,) + rows.shape[levels + 1 :])

    projected = jnp.concatenate(
        [
            in_order(jnp.einsum("...d,dn->...n", stacked, zx_weight, preferred_element_type=jnp.float32)),
            in_order(jnp.einsum("...d,dn->...n", stacked, step_weight, preferred_element_type=jnp.float32)),
        ],
        axis=1,
    ).astype(jnp.bfloat16)
    gate_raw = projected[:, :inner_dev]
    inner_raw = projected[:, inner_dev : 2 * inner_dev]
    step_raw = projected[:, 2 * inner_dev :]
    own_maps = jnp.einsum(
        "...d,sgd->...gs", stacked, group_weight, preferred_element_type=jnp.float32
    ).astype(jnp.bfloat16)
    own_maps = jnp.moveaxis(in_order(own_maps), 1, 0)
    own_maps = jnp.broadcast_to(own_maps[:, None], (GROUPS, per_group_dev) + own_maps.shape[1:])
    own_maps = own_maps.reshape((tp_size,) + own_maps.shape[2:])
    got_maps = lax.all_to_all(own_maps, "tp", 0, 0, tiled=True)
    map_part = jnp.transpose(got_maps, (1, 0, 2)).reshape(length, group_cols)
    border_rows = KERNEL - 1
    prior = shifted(
        jnp.concatenate([inner_raw[length - border_rows :], map_part[length - border_rows :]], axis=1),
        "ctx",
        1,
    )
    inner_prior = prior[:, :inner_dev]
    map_prior = prior[:, inner_dev:]
    x_conv = causal_conv(inner_prior, inner_raw, conv_inner, inner_bias)
    own_taps = lax.dynamic_slice_in_dim(conv_group, group_index * group_cols, group_cols, 1)
    own_bias = lax.dynamic_slice_in_dim(group_bias, group_index * group_cols, group_cols, 0)
    maps = causal_conv(map_prior, map_part, own_taps, own_bias)
    step_size = jax.nn.softplus(step_raw.astype(jnp.float32) + step_bias[None, :])
    decay_rate = -jnp.exp(log_rate)
    blocks = length // BLOCK
    x_blocks = x_conv.reshape(blocks, BLOCK, heads_dev, HEAD_DIM)
    input_map = maps[:, :STATE].reshape(blocks, BLOCK, STATE)
    output_map = maps[:, STATE:].reshape(blocks, BLOCK, STATE)
    step_blocks = jnp.swapaxes(step_size.reshape(blocks, BLOCK, heads_dev), 1, 2)
    cumulative = jnp.cumsum(step_blocks * decay_rate[None, :, None], axis=2)
    scores = jnp.einsum("kin,kjn->kij", output_map, input_map, preferred_element_type=jnp.float32)
    causal = jnp.arange(BLOCK)[:, None] >= jnp.arange(BLOCK)[None, :]
    exponent = jnp.where(causal, cumulative[..., :, None] - cumulative[..., None, :], -jnp.inf)
    mixing = (scores[:, None] * jnp.exp(exponent) * step_blocks[..., None, :]).astype(jnp.bfloat16)
    within = jnp.einsum("khij,kjhp->kihp", mixing, x_blocks, preferred_element_type=jnp.float32)
    weight = jnp.exp(cumulative[..., BLOCK - 1 :] - cumulative) * step_blocks
    x_float = x_blocks.astype(jnp.float32)
    weighted = (x_float * jnp.swapaxes(weight, 1, 2)[..., None]).astype(jnp.bfloat16)
    block_state = jnp.einsum(
        "kjhp,kjn->khpn", weighted, input_map, preferred_element_type=jnp.float32
    )
    block_decay = jnp.exp(cumulative[..., BLOCK - 1])

    def advance(carry, item):
        running, product = carry
        block_stop_index, state_here = item
        return (
            (block_stop_index[:, None, None] * running + state_here, product * block_stop_index),
            (running, product),
        )

    empty_state = jnp.zeros((heads_dev, HEAD_DIM, STATE), jnp.float32)
    (dev_state, dev_decay), (local_starts, prefixes) = lax.scan(
        advance, (empty_state, jnp.ones((heads_dev,), jnp.float32)), (block_decay, block_state)
    )
    ctx_size = lax.axis_size("ctx")
    place = lax.axis_index("ctx")
    in_decay = jnp.ones_like(dev_decay)
    in_state = jnp.zeros_like(dev_state)
    run_decay = dev_decay
    run_state = dev_state
    reach = 1
    while reach < ctx_size:
        packed = jnp.concatenate(
            [run_state, jnp.broadcast_to(run_decay[:, None, None], (heads_dev, 1, STATE))], axis=1
        )
        got = shifted(packed, "ctx", reach)
        valid = place >= reach
        got_state = jnp.where(valid, got[:, :HEAD_DIM], 0.0)
        got_decay = jnp.where(valid, got[:, HEAD_DIM, 0], 1.0)
        in_state = in_decay[:, None, None] * got_state + in_state
        in_decay = got_decay * in_decay
        run_state = run_decay[:, None, None] * got_state + run_state
        run_decay = got_decay * run_decay
        reach *= 2
    incoming = in_state
    starting = local_starts + prefixes[:, :, None, None] * incoming[None]
    carried = jnp.einsum(
        "kin,khpn->kihp",
        output_map,
        starting.astype(jnp.bfloat16),
        preferred_element_type=jnp.float32,
    )
    carried = carried * jnp.swapaxes(jnp.exp(cumulative), 1, 2)[..., None]
    result_heads = within + carried + skip_weight[None, None, :, None] * x_float
    result_heads = result_heads.reshape(length, inner_dev)
    gated = result_heads * jax.nn.silu(gate_raw.astype(jnp.float32))
    total = jnp.sum(gated * gated, axis=1)
    bit = 1
    while bit < per_group_dev:
        total = total + swapped(total, "tp", bit)
        bit *= 2
    scaled = (gated * norm_gain[None, :]).astype(jnp.bfloat16)
    scaled = scaled.reshape((2,) * levels + (length // tp_size, inner_dev))
    scaled = jnp.transpose(scaled, flipped + (levels, levels + 1))
    partial = jnp.einsum("...c,cn->...n", scaled, out_weight, preferred_element_type=jnp.float32)
    within_bits = [bit for bit in tp_bits if bit < per_group_dev]
    across_bits = [bit for bit in tp_bits if bit >= per_group_dev]
    held = halve(partial, "tp", within_bits)
    inverse = lax.rsqrt(total / (HEADS * HEAD_DIM // GROUPS) + 1e-05)
    inverse = jnp.transpose(inverse.reshape((2,) * levels + (length // tp_size,)), flipped + (levels,))
    for bit in within_bits:
        inverse = lax.dynamic_index_in_dim(inverse, (lax.axis_index("tp") // bit) % 2, 0, keepdims=False)
    held = held * inverse[..., None]
    held = halve(held, "tp", across_bits)
    mixed = held
    return mixed.astype(jnp.bfloat16)


def solution(mesh):
    placed = (
        P(("ctx", "tp"), None),
        P(None, None, "tp"),
        P(None, "tp"),
        P("tp", None, None),
        P(None, "tp"),
        P("tp"),
        P(),
        P(),
        P("tp"),
        P("tp"),
        P("tp"),
        P("tp"),
        P("tp", None),
    )
    return jax.shard_map(
        body, mesh=mesh, in_specs=placed, out_specs=P(("ctx", "tp"), None), check_vma=False
    )
```

```python
import jax
import jax.numpy as jnp
from jax import lax
from jax.sharding import PartitionSpec as P

HEADS = 64
HEAD_DIM = 64
STATE = 128
GROUPS = 4
BLOCK = 256
KERNEL = 4


def shifted(x, axis, by):
    peers = lax.axis_size(axis)
    pairs = [(i, i + by) for i in range(peers) if 0 <= i + by < peers]
    return lax.ppermute(x, axis, pairs)


def swapped(x, axis, bit):
    peers = lax.axis_size(axis)
    return lax.ppermute(x, axis, [(i, i ^ bit) for i in range(peers)])


def gather_rows(rows, axis, bits):
    place = lax.axis_index(axis)
    peers = lax.axis_size(axis)
    held = rows
    for bit in reversed(bits):
        other = swapped(held, axis, bit)
        low = (place & bit) == 0
        held = jnp.where(low, jnp.stack([held, other]), jnp.stack([other, held]))
    return held


def halve(held, axis, bits):
    place = lax.axis_index(axis)
    for bit in bits:
        mine = (place // bit) % 2
        keep = lax.dynamic_index_in_dim(held, mine, 0, keepdims=False)
        give = lax.dynamic_index_in_dim(held, 1 - mine, 0, keepdims=False)
        held = keep + swapped(give.astype(jnp.bfloat16), axis, bit).astype(jnp.float32)
    return held


def causal_conv(prior_rows, raw_rows, conv_weight, conv_bias):
    joined = jnp.concatenate([prior_rows, raw_rows], axis=0).astype(jnp.float32)
    length = raw_rows.shape[0]
    running = jnp.broadcast_to(conv_bias[None, :], raw_rows.shape)
    for offset in range(conv_weight.shape[0]):
        running = running + conv_weight[offset][None, :] * joined[offset : offset + length]
    return jax.nn.silu(running).astype(jnp.bfloat16)


def body(
    hidden,
    in_weight,
    step_weight,
    group_weight,
    conv_inner,
    inner_bias,
    conv_group,
    group_bias,
    step_bias,
    log_rate,
    skip_weight,
    norm_gain,
    out_weight,
):
    tp_size = lax.axis_size("tp")
    tp_bits = [1 << k for k in range(tp_size.bit_length() - 1)]
    heads_dev = log_rate.shape[0]
    inner_dev = in_weight.shape[2]
    group_cols = 2 * STATE
    per_group_dev = (HEADS // GROUPS) // heads_dev
    group_index = lax.axis_index("tp") // per_group_dev
    zx_weight = in_weight.reshape(in_weight.shape[0], 2 * inner_dev)
    stacked = gather_rows(hidden, "tp", tp_bits)
    levels = len(tp_bits)
    length = tp_size * hidden.shape[0]
    flipped = tuple(reversed(range(levels)))

    def in_order(rows):
        rows = jnp.transpose(rows, flipped + tuple(range(levels, rows.ndim)))
        return rows.reshape((length,) + rows.shape[levels + 1 :])

    projected = jnp.concatenate(
        [
            in_order(jnp.einsum("...d,dn->...n", stacked, zx_weight, preferred_element_type=jnp.float32)),
            in_order(jnp.einsum("...d,dn->...n", stacked, step_weight, preferred_element_type=jnp.float32)),
        ],
        axis=1,
    ).astype(jnp.bfloat16)
    gate_raw = projected[:, :inner_dev]
    inner_raw = projected[:, inner_dev : 2 * inner_dev]
    step_raw = projected[:, 2 * inner_dev :]
    own_group = jnp.broadcast_to(
        jnp.swapaxes(group_weight, 0, 1)[:, None], (GROUPS, per_group_dev) + group_weight[:, 0].shape
    ).reshape((tp_size,) + group_weight[:, 0].shape)
    map_weight = lax.all_to_all(own_group, "tp", 0, 0, tiled=True)
    map_weight = map_weight.reshape((-1,) + map_weight.shape[2:])
    map_part = in_order(
        jnp.einsum("...d,sd->...s", stacked, map_weight, preferred_element_type=jnp.float32)
    ).astype(jnp.bfloat16)
    border_rows = KERNEL - 1
    last_rows = stacked[(1,) * levels][hidden.shape[0] - border_rows :]
    before = shifted(last_rows, "ctx", 1)
    inner_prior = jnp.dot(
        before, zx_weight[:, inner_dev:], preferred_element_type=jnp.float32
    ).astype(jnp.bfloat16)
    map_prior = lax.dot_general(
        before, map_weight, (((1,), (1,)), ((), ())), preferred_element_type=jnp.float32
    ).astype(jnp.bfloat16)
    x_conv = causal_conv(inner_prior, inner_raw, conv_inner, inner_bias)
    own_taps = lax.dynamic_slice_in_dim(conv_group, group_index * group_cols, group_cols, 1)
    own_bias = lax.dynamic_slice_in_dim(group_bias, group_index * group_cols, group_cols, 0)
    maps = causal_conv(map_prior, map_part, own_taps, own_bias)
    step_size = jax.nn.softplus(step_raw.astype(jnp.float32) + step_bias[None, :])
    decay_rate = -jnp.exp(log_rate)
    blocks = length // BLOCK
    x_blocks = x_conv.reshape(blocks, BLOCK, heads_dev, HEAD_DIM)
    input_map = maps[:, :STATE].reshape(blocks, BLOCK, STATE)
    output_map = maps[:, STATE:].reshape(blocks, BLOCK, STATE)
    step_blocks = jnp.swapaxes(step_size.reshape(blocks, BLOCK, heads_dev), 1, 2)
    cumulative = jnp.cumsum(step_blocks * decay_rate[None, :, None], axis=2)
    scores = jnp.einsum("kin,kjn->kij", output_map, input_map, preferred_element_type=jnp.float32)
    causal = jnp.arange(BLOCK)[:, None] >= jnp.arange(BLOCK)[None, :]
    exponent = jnp.where(causal, cumulative[..., :, None] - cumulative[..., None, :], -jnp.inf)
    mixing = (scores[:, None] * jnp.exp(exponent) * step_blocks[..., None, :]).astype(jnp.bfloat16)
    within = jnp.einsum("khij,kjhp->kihp", mixing, x_blocks, preferred_element_type=jnp.float32)
    weight = jnp.exp(cumulative[..., BLOCK - 1 :] - cumulative) * step_blocks
    x_float = x_blocks.astype(jnp.float32)
    weighted = (x_float * jnp.swapaxes(weight, 1, 2)[..., None]).astype(jnp.bfloat16)
    block_state = jnp.einsum(
        "kjhp,kjn->khpn", weighted, input_map, preferred_element_type=jnp.float32
    )
    block_decay = jnp.exp(cumulative[..., BLOCK - 1])

    def advance(carry, item):
        running, product = carry
        block_stop_index, state_here = item
        return (
            (block_stop_index[:, None, None] * running + state_here, product * block_stop_index),
            (running, product),
        )

    empty_state = jnp.zeros((heads_dev, HEAD_DIM, STATE), jnp.float32)
    (dev_state, dev_decay), (local_starts, prefixes) = lax.scan(
        advance, (empty_state, jnp.ones((heads_dev,), jnp.float32)), (block_decay, block_state)
    )
    ctx_size = lax.axis_size("ctx")
    place = lax.axis_index("ctx")
    in_decay = jnp.ones_like(dev_decay)
    in_state = jnp.zeros_like(dev_state)
    run_decay = dev_decay
    run_state = dev_state
    reach = 1
    while reach < ctx_size:
        packed = jnp.concatenate(
            [run_state, jnp.broadcast_to(run_decay[:, None, None], (heads_dev, 1, STATE))], axis=1
        )
        got = shifted(packed, "ctx", reach)
        valid = place >= reach
        got_state = jnp.where(valid, got[:, :HEAD_DIM], 0.0)
        got_decay = jnp.where(valid, got[:, HEAD_DIM, 0], 1.0)
        in_state = in_decay[:, None, None] * got_state + in_state
        in_decay = got_decay * in_decay
        run_state = run_decay[:, None, None] * got_state + run_state
        run_decay = got_decay * run_decay
        reach *= 2
    incoming = in_state
    starting = local_starts + prefixes[:, :, None, None] * incoming[None]
    carried = jnp.einsum(
        "kin,khpn->kihp",
        output_map,
        starting.astype(jnp.bfloat16),
        preferred_element_type=jnp.float32,
    )
    carried = carried * jnp.swapaxes(jnp.exp(cumulative), 1, 2)[..., None]
    result_heads = within + carried + skip_weight[None, None, :, None] * x_float
    result_heads = result_heads.reshape(length, inner_dev)
    gated = result_heads * jax.nn.silu(gate_raw.astype(jnp.float32))
    total = jnp.sum(gated * gated, axis=1)
    bit = 1
    while bit < per_group_dev:
        total = total + swapped(total, "tp", bit)
        bit *= 2
    scaled = (gated * norm_gain[None, :]).astype(jnp.bfloat16)
    scaled = scaled.reshape((2,) * levels + (length // tp_size, inner_dev))
    scaled = jnp.transpose(scaled, flipped + (levels, levels + 1))
    partial = jnp.einsum("...c,cn->...n", scaled, out_weight, preferred_element_type=jnp.float32)
    within_bits = [bit for bit in tp_bits if bit < per_group_dev]
    across_bits = [bit for bit in tp_bits if bit >= per_group_dev]
    held = halve(partial, "tp", within_bits)
    inverse = lax.rsqrt(total / (HEADS * HEAD_DIM // GROUPS) + 1e-05)
    inverse = jnp.transpose(inverse.reshape((2,) * levels + (length // tp_size,)), flipped + (levels,))
    for bit in within_bits:
        inverse = lax.dynamic_index_in_dim(inverse, (lax.axis_index("tp") // bit) % 2, 0, keepdims=False)
    held = held * inverse[..., None]
    held = halve(held, "tp", across_bits)
    mixed = held
    return mixed.astype(jnp.bfloat16)


def solution(mesh):
    placed = (
        P(("ctx", "tp"), None),
        P(None, None, "tp"),
        P(None, "tp"),
        P("tp", None, None),
        P(None, "tp"),
        P("tp"),
        P(),
        P(),
        P("tp"),
        P("tp"),
        P("tp"),
        P("tp"),
        P("tp", None),
    )
    return jax.shard_map(
        body, mesh=mesh, in_specs=placed, out_specs=P(("ctx", "tp"), None), check_vma=False
    )
```

```python
import jax
import jax.numpy as jnp
from jax import lax
from jax.sharding import PartitionSpec as P

HEADS = 64
HEAD_DIM = 64
STATE = 128
GROUPS = 4
BLOCK = 256
KERNEL = 4


def shifted(x, axis, by):
    peers = lax.axis_size(axis)
    pairs = [(i, i + by) for i in range(peers) if 0 <= i + by < peers]
    return lax.ppermute(x, axis, pairs)


def swapped(x, axis, offset):
    peers = lax.axis_size(axis)
    return lax.ppermute(x, axis, [(i, i ^ offset) for i in range(peers)])


def digits_of(size, shift=0):
    found = []
    while size > 1:
        radix = 4 if size % 4 == 0 else 2
        found.append((shift, radix))
        shift += radix.bit_length() - 1
        size //= radix
    return found


def gather_rows(rows, axis, digits):
    place = lax.axis_index(axis)
    held = rows
    for shift, radix in reversed(digits):
        mine = (place >> shift) % radix
        by_offset = jnp.stack([held] + [swapped(held, axis, o << shift) for o in range(1, radix)])
        held = jnp.stack(
            [lax.dynamic_index_in_dim(by_offset, j ^ mine, 0, keepdims=False) for j in range(radix)]
        )
    return held


def scatter_sum(held, axis, digits):
    place = lax.axis_index(axis)
    for shift, radix in digits:
        mine = (place >> shift) % radix
        total = lax.dynamic_index_in_dim(held, mine, 0, keepdims=False)
        for o in range(1, radix):
            give = lax.dynamic_index_in_dim(held, mine ^ o, 0, keepdims=False)
            total = total + swapped(give.astype(jnp.bfloat16), axis, o << shift).astype(jnp.float32)
        held = total
    return held


def causal_conv(prior_rows, raw_rows, conv_weight, conv_bias):
    joined = jnp.concatenate([prior_rows, raw_rows], axis=0).astype(jnp.float32)
    length = raw_rows.shape[0]
    running = jnp.broadcast_to(conv_bias[None, :], raw_rows.shape)
    for offset in range(conv_weight.shape[0]):
        running = running + conv_weight[offset][None, :] * joined[offset : offset + length]
    return jax.nn.silu(running).astype(jnp.bfloat16)


def body(
    hidden,
    in_weight,
    step_weight,
    group_weight,
    conv_inner,
    inner_bias,
    conv_group,
    group_bias,
    step_bias,
    log_rate,
    skip_weight,
    norm_gain,
    out_weight,
):
    tp_size = lax.axis_size("tp")
    heads_dev = log_rate.shape[0]
    inner_dev = in_weight.shape[2]
    group_cols = 2 * STATE
    per_group_dev = (HEADS // GROUPS) // heads_dev
    within_digits = digits_of(per_group_dev)
    across_digits = digits_of(tp_size // per_group_dev, per_group_dev.bit_length() - 1)
    tp_digits = within_digits + across_digits
    group_index = lax.axis_index("tp") // per_group_dev
    zx_weight = in_weight.reshape(in_weight.shape[0], 2 * inner_dev)
    stacked = gather_rows(hidden, "tp", tp_digits)
    levels = len(tp_digits)
    length = tp_size * hidden.shape[0]
    flipped = tuple(reversed(range(levels)))

    def in_order(rows):
        rows = jnp.transpose(rows, flipped + tuple(range(levels, rows.ndim)))
        return rows.reshape((length,) + rows.shape[levels + 1 :])

    projected = jnp.concatenate(
        [
            in_order(jnp.einsum("...d,dn->...n", stacked, zx_weight, preferred_element_type=jnp.float32)),
            in_order(jnp.einsum("...d,dn->...n", stacked, step_weight, preferred_element_type=jnp.float32)),
        ],
        axis=1,
    ).astype(jnp.bfloat16)
    gate_raw = projected[:, :inner_dev]
    inner_raw = projected[:, inner_dev : 2 * inner_dev]
    step_raw = projected[:, 2 * inner_dev :]
    own_maps = jnp.einsum(
        "...d,sgd->...gs", stacked, group_weight, preferred_element_type=jnp.float32
    ).astype(jnp.bfloat16)
    own_maps = jnp.moveaxis(in_order(own_maps), 1, 0)
    own_maps = jnp.broadcast_to(own_maps[:, None], (GROUPS, per_group_dev) + own_maps.shape[1:])
    own_maps = own_maps.reshape((tp_size,) + own_maps.shape[2:])
    got_maps = lax.all_to_all(own_maps, "tp", 0, 0, tiled=True)
    map_part = jnp.transpose(got_maps, (1, 0, 2)).reshape(length, group_cols)
    border_rows = KERNEL - 1
    prior = shifted(
        jnp.concatenate([inner_raw[length - border_rows :], map_part[length - border_rows :]], axis=1),
        "ctx",
        1,
    )
    inner_prior = prior[:, :inner_dev]
    map_prior = prior[:, inner_dev:]
    x_conv = causal_conv(inner_prior, inner_raw, conv_inner, inner_bias)
    own_taps = lax.dynamic_slice_in_dim(conv_group, group_index * group_cols, group_cols, 1)
    own_bias = lax.dynamic_slice_in_dim(group_bias, group_index * group_cols, group_cols, 0)
    maps = causal_conv(map_prior, map_part, own_taps, own_bias)
    step_size = jax.nn.softplus(step_raw.astype(jnp.float32) + step_bias[None, :])
    decay_rate = -jnp.exp(log_rate)
    blocks = length // BLOCK
    x_blocks = x_conv.reshape(blocks, BLOCK, heads_dev, HEAD_DIM)
    input_map = maps[:, :STATE].reshape(blocks, BLOCK, STATE)
    output_map = maps[:, STATE:].reshape(blocks, BLOCK, STATE)
    step_blocks = jnp.swapaxes(step_size.reshape(blocks, BLOCK, heads_dev), 1, 2)
    cumulative = jnp.cumsum(step_blocks * decay_rate[None, :, None], axis=2)
    scores = jnp.einsum("kin,kjn->kij", output_map, input_map, preferred_element_type=jnp.float32)
    causal = jnp.arange(BLOCK)[:, None] >= jnp.arange(BLOCK)[None, :]
    exponent = jnp.where(causal, cumulative[..., :, None] - cumulative[..., None, :], -jnp.inf)
    mixing = (scores[:, None] * jnp.exp(exponent) * step_blocks[..., None, :]).astype(jnp.bfloat16)
    within = jnp.einsum("khij,kjhp->kihp", mixing, x_blocks, preferred_element_type=jnp.float32)
    weight = jnp.exp(cumulative[..., BLOCK - 1 :] - cumulative) * step_blocks
    x_float = x_blocks.astype(jnp.float32)
    weighted = (x_float * jnp.swapaxes(weight, 1, 2)[..., None]).astype(jnp.bfloat16)
    block_state = jnp.einsum(
        "kjhp,kjn->khpn", weighted, input_map, preferred_element_type=jnp.float32
    )
    block_decay = jnp.exp(cumulative[..., BLOCK - 1])

    def advance(carry, item):
        running, product = carry
        block_stop_index, state_here = item
        return (
            (block_stop_index[:, None, None] * running + state_here, product * block_stop_index),
            (running, product),
        )

    empty_state = jnp.zeros((heads_dev, HEAD_DIM, STATE), jnp.float32)
    (dev_state, dev_decay), (local_starts, prefixes) = lax.scan(
        advance, (empty_state, jnp.ones((heads_dev,), jnp.float32)), (block_decay, block_state)
    )
    ctx_size = lax.axis_size("ctx")
    place = lax.axis_index("ctx")
    in_decay = jnp.ones_like(dev_decay)
    in_state = jnp.zeros_like(dev_state)
    run_decay = dev_decay
    run_state = dev_state
    reach = 1
    while reach < ctx_size:
        radix = 4 if (ctx_size // reach) % 4 == 0 else 2
        packed = jnp.concatenate(
            [run_state, jnp.broadcast_to(run_decay[:, None, None], (heads_dev, 1, STATE))], axis=1
        )
        arrived = [shifted(packed, "ctx", m * reach) for m in range(1, radix)]
        for m, got in zip(range(1, radix), arrived):
            valid = place >= m * reach
            got_state = jnp.where(valid, got[:, :HEAD_DIM], 0.0)
            got_decay = jnp.where(valid, got[:, HEAD_DIM, 0], 1.0)
            in_state = in_decay[:, None, None] * got_state + in_state
            in_decay = got_decay * in_decay
            run_state = run_decay[:, None, None] * got_state + run_state
            run_decay = got_decay * run_decay
        reach *= radix
    incoming = in_state
    starting = local_starts + prefixes[:, :, None, None] * incoming[None]
    carried = jnp.einsum(
        "kin,khpn->kihp",
        output_map,
        starting.astype(jnp.bfloat16),
        preferred_element_type=jnp.float32,
    )
    carried = carried * jnp.swapaxes(jnp.exp(cumulative), 1, 2)[..., None]
    result_heads = within + carried + skip_weight[None, None, :, None] * x_float
    result_heads = result_heads.reshape(length, inner_dev)
    gated = result_heads * jax.nn.silu(gate_raw.astype(jnp.float32))
    squares = jnp.sum(gated * gated, axis=1)
    total = squares
    for shift, radix in within_digits:
        total = total + sum(swapped(total, "tp", o << shift) for o in range(1, radix))
    radices = tuple(radix for _, radix in reversed(tp_digits))
    scaled = (gated * norm_gain[None, :]).astype(jnp.bfloat16)
    scaled = scaled.reshape(radices + (length // tp_size, inner_dev))
    scaled = jnp.transpose(scaled, flipped + (levels, levels + 1))
    partial = jnp.einsum("...c,cn->...n", scaled, out_weight, preferred_element_type=jnp.float32)
    held = scatter_sum(partial, "tp", within_digits)
    inverse = lax.rsqrt(total / (HEADS * HEAD_DIM // GROUPS) + 1e-05)
    inverse = jnp.transpose(inverse.reshape(radices + (length // tp_size,)), flipped + (levels,))
    for shift, radix in within_digits:
        mine = (lax.axis_index("tp") >> shift) % radix
        inverse = lax.dynamic_index_in_dim(inverse, mine, 0, keepdims=False)
    held = held * inverse[..., None]
    mixed = scatter_sum(held, "tp", across_digits)
    return mixed.astype(jnp.bfloat16)


def solution(mesh):
    placed = (
        P(("ctx", "tp"), None),
        P(None, None, "tp"),
        P(None, "tp"),
        P("tp", None, None),
        P(None, "tp"),
        P("tp"),
        P(),
        P(),
        P("tp"),
        P("tp"),
        P("tp"),
        P("tp"),
        P("tp", None),
    )
    return jax.shard_map(
        body, mesh=mesh, in_specs=placed, out_specs=P(("ctx", "tp"), None), check_vma=False
    )
```

```python
import jax
import jax.numpy as jnp
from jax import lax
from jax.sharding import PartitionSpec as P

HEADS = 64
HEAD_DIM = 64
STATE = 128
GROUPS = 4
BLOCK = 256
KERNEL = 4


def shifted(x, axis, by):
    peers = lax.axis_size(axis)
    pairs = [(i, i + by) for i in range(peers) if 0 <= i + by < peers]
    return lax.ppermute(x, axis, pairs)


def swapped(x, axis, bit):
    peers = lax.axis_size(axis)
    return lax.ppermute(x, axis, [(i, i ^ bit) for i in range(peers)])


def gather_rows(rows, axis, bits):
    place = lax.axis_index(axis)
    peers = lax.axis_size(axis)
    held = rows
    for bit in reversed(bits):
        other = swapped(held, axis, bit)
        low = (place & bit) == 0
        held = jnp.where(low, jnp.stack([held, other]), jnp.stack([other, held]))
    return held


def halve(held, axis, bits):
    place = lax.axis_index(axis)
    for bit in bits:
        mine = (place // bit) % 2
        keep = lax.dynamic_index_in_dim(held, mine, 0, keepdims=False)
        give = lax.dynamic_index_in_dim(held, 1 - mine, 0, keepdims=False)
        held = keep + swapped(give.astype(jnp.bfloat16), axis, bit).astype(jnp.float32)
    return held


def causal_conv(prior_rows, raw_rows, conv_weight, conv_bias):
    joined = jnp.concatenate([prior_rows, raw_rows], axis=0).astype(jnp.float32)
    length = raw_rows.shape[0]
    running = jnp.broadcast_to(conv_bias[None, :], raw_rows.shape)
    for offset in range(conv_weight.shape[0]):
        running = running + conv_weight[offset][None, :] * joined[offset : offset + length]
    return jax.nn.silu(running).astype(jnp.bfloat16)


def body(
    hidden,
    in_weight,
    step_weight,
    group_weight,
    conv_inner,
    inner_bias,
    conv_group,
    group_bias,
    step_bias,
    log_rate,
    skip_weight,
    norm_gain,
    out_weight,
):
    tp_size = lax.axis_size("tp")
    tp_bits = [1 << k for k in range(tp_size.bit_length() - 1)]
    heads_dev = log_rate.shape[0]
    inner_dev = in_weight.shape[2]
    group_cols = 2 * STATE
    per_group_dev = (HEADS // GROUPS) // heads_dev
    group_index = lax.axis_index("tp") // per_group_dev
    zx_weight = in_weight.reshape(in_weight.shape[0], 2 * inner_dev)
    stacked = gather_rows(hidden, "tp", tp_bits)
    levels = len(tp_bits)
    length = tp_size * hidden.shape[0]
    flipped = tuple(reversed(range(levels)))

    def in_order(rows):
        rows = jnp.transpose(rows, flipped + tuple(range(levels, rows.ndim)))
        return rows.reshape((length,) + rows.shape[levels + 1 :])

    projected = jnp.concatenate(
        [
            in_order(jnp.einsum("...d,dn->...n", stacked, zx_weight, preferred_element_type=jnp.float32)),
            in_order(jnp.einsum("...d,dn->...n", stacked, step_weight, preferred_element_type=jnp.float32)),
        ],
        axis=1,
    ).astype(jnp.bfloat16)
    gate_raw = projected[:, :inner_dev]
    inner_raw = projected[:, inner_dev : 2 * inner_dev]
    step_raw = projected[:, 2 * inner_dev :]
    own_maps = jnp.einsum(
        "...d,sgd->...gs", stacked, group_weight, preferred_element_type=jnp.float32
    ).astype(jnp.bfloat16)
    own_maps = jnp.moveaxis(in_order(own_maps), 1, 0)
    own_maps = jnp.broadcast_to(own_maps[:, None], (GROUPS, per_group_dev) + own_maps.shape[1:])
    own_maps = own_maps.reshape((tp_size,) + own_maps.shape[2:])
    got_maps = lax.all_to_all(own_maps, "tp", 0, 0, tiled=True)
    map_part = jnp.transpose(got_maps, (1, 0, 2)).reshape(length, group_cols)
    border_rows = KERNEL - 1
    prior = shifted(
        jnp.concatenate([inner_raw[length - border_rows :], map_part[length - border_rows :]], axis=1),
        "ctx",
        1,
    )
    inner_prior = prior[:, :inner_dev]
    map_prior = prior[:, inner_dev:]
    x_conv = causal_conv(inner_prior, inner_raw, conv_inner, inner_bias)
    own_taps = lax.dynamic_slice_in_dim(conv_group, group_index * group_cols, group_cols, 1)
    own_bias = lax.dynamic_slice_in_dim(group_bias, group_index * group_cols, group_cols, 0)
    maps = causal_conv(map_prior, map_part, own_taps, own_bias)
    step_size = jax.nn.softplus(step_raw.astype(jnp.float32) + step_bias[None, :])
    decay_rate = -jnp.exp(log_rate)
    blocks = length // BLOCK
    x_blocks = x_conv.reshape(blocks, BLOCK, heads_dev, HEAD_DIM)
    input_map = maps[:, :STATE].reshape(blocks, BLOCK, STATE)
    output_map = maps[:, STATE:].reshape(blocks, BLOCK, STATE)
    step_blocks = jnp.swapaxes(step_size.reshape(blocks, BLOCK, heads_dev), 1, 2)
    cumulative = jnp.cumsum(step_blocks * decay_rate[None, :, None], axis=2)
    scores = jnp.einsum("kin,kjn->kij", output_map, input_map, preferred_element_type=jnp.float32)
    causal = jnp.arange(BLOCK)[:, None] >= jnp.arange(BLOCK)[None, :]
    exponent = jnp.where(causal, cumulative[..., :, None] - cumulative[..., None, :], -jnp.inf)
    mixing = (scores[:, None] * jnp.exp(exponent) * step_blocks[..., None, :]).astype(jnp.bfloat16)
    within = jnp.einsum("khij,kjhp->kihp", mixing, x_blocks, preferred_element_type=jnp.float32)
    weight = jnp.exp(cumulative[..., BLOCK - 1 :] - cumulative) * step_blocks
    x_float = x_blocks.astype(jnp.float32)
    weighted = (x_float * jnp.swapaxes(weight, 1, 2)[..., None]).astype(jnp.bfloat16)
    block_state = jnp.einsum(
        "kjhp,kjn->khpn", weighted, input_map, preferred_element_type=jnp.float32
    )
    block_decay = jnp.exp(cumulative[..., BLOCK - 1])

    def advance(carry, item):
        running, product = carry
        block_stop_index, state_here = item
        return (
            (block_stop_index[:, None, None] * running + state_here, product * block_stop_index),
            (running, product),
        )

    empty_state = jnp.zeros((heads_dev, HEAD_DIM, STATE), jnp.float32)
    (dev_state, dev_decay), (local_starts, prefixes) = lax.scan(
        advance, (empty_state, jnp.ones((heads_dev,), jnp.float32)), (block_decay, block_state)
    )
    ctx_size = lax.axis_size("ctx")
    place = lax.axis_index("ctx")
    in_decay = jnp.ones_like(dev_decay)
    in_state = jnp.zeros_like(dev_state)
    run_decay = dev_decay
    run_state = dev_state
    reach = 1
    while reach < ctx_size:
        packed = jnp.concatenate(
            [run_state, jnp.broadcast_to(run_decay[:, None, None], (heads_dev, 1, STATE))], axis=1
        )
        got = shifted(packed.astype(jnp.bfloat16), "ctx", reach).astype(jnp.float32)
        valid = place >= reach
        got_state = jnp.where(valid, got[:, :HEAD_DIM], 0.0)
        got_decay = jnp.where(valid, got[:, HEAD_DIM, 0], 1.0)
        in_state = in_decay[:, None, None] * got_state + in_state
        in_decay = got_decay * in_decay
        run_state = run_decay[:, None, None] * got_state + run_state
        run_decay = got_decay * run_decay
        reach *= 2
    incoming = in_state
    starting = local_starts + prefixes[:, :, None, None] * incoming[None]
    carried = jnp.einsum(
        "kin,khpn->kihp",
        output_map,
        starting.astype(jnp.bfloat16),
        preferred_element_type=jnp.float32,
    )
    carried = carried * jnp.swapaxes(jnp.exp(cumulative), 1, 2)[..., None]
    result_heads = within + carried + skip_weight[None, None, :, None] * x_float
    result_heads = result_heads.reshape(length, inner_dev)
    gated = result_heads * jax.nn.silu(gate_raw.astype(jnp.float32))
    scaled = jnp.concatenate(
        [(gated * norm_gain[None, :]).astype(jnp.bfloat16), (gated * gated).astype(jnp.bfloat16)], axis=1
    )
    width = out_weight.shape[1]
    extended = jnp.concatenate(
        [
            jnp.concatenate([out_weight, jnp.zeros((inner_dev, 128), out_weight.dtype)], axis=1),
            jnp.concatenate(
                [jnp.zeros((inner_dev, width), out_weight.dtype), jnp.ones((inner_dev, 128), out_weight.dtype)],
                axis=1,
            ),
        ],
        axis=0,
    )
    scaled = scaled.reshape((2,) * levels + (length // tp_size, 2 * inner_dev))
    scaled = jnp.transpose(scaled, flipped + (levels, levels + 1))
    partial = jnp.einsum("...c,cn->...n", scaled, extended, preferred_element_type=jnp.float32)
    within_bits = [bit for bit in tp_bits if bit < per_group_dev]
    across_bits = [bit for bit in tp_bits if bit >= per_group_dev]
    held = halve(partial, "tp", within_bits)
    inverse = lax.rsqrt(held[..., width] / (HEADS * HEAD_DIM // GROUPS) + 1e-05)
    held = held[..., :width] * inverse[..., None]
    held = halve(held, "tp", across_bits)
    mixed = held
    return mixed.astype(jnp.bfloat16)


def solution(mesh):
    placed = (
        P(("ctx", "tp"), None),
        P(None, None, "tp"),
        P(None, "tp"),
        P("tp", None, None),
        P(None, "tp"),
        P("tp"),
        P(),
        P(),
        P("tp"),
        P("tp"),
        P("tp"),
        P("tp"),
        P("tp", None),
    )
    return jax.shard_map(
        body, mesh=mesh, in_specs=placed, out_specs=P(("ctx", "tp"), None), check_vma=False
    )
```

```python
import jax
import jax.numpy as jnp
from jax import lax
from jax.sharding import PartitionSpec as P

HEADS = 64
HEAD_DIM = 64
STATE = 128
GROUPS = 4
BLOCK = 256
KERNEL = 4


def shifted(x, axis, by):
    peers = lax.axis_size(axis)
    pairs = [(i, i + by) for i in range(peers) if 0 <= i + by < peers]
    return lax.ppermute(x, axis, pairs)


def swapped(x, axis, bit):
    peers = lax.axis_size(axis)
    return lax.ppermute(x, axis, [(i, i ^ bit) for i in range(peers)])


def gather_rows(rows, axis, bits):
    place = lax.axis_index(axis)
    peers = lax.axis_size(axis)
    held = rows
    for bit in reversed(bits):
        other = swapped(held, axis, bit)
        low = (place & bit) == 0
        held = jnp.where(low, jnp.stack([held, other]), jnp.stack([other, held]))
    return held


def halve(held, axis, bits):
    place = lax.axis_index(axis)
    for bit in bits:
        mine = (place // bit) % 2
        keep = lax.dynamic_index_in_dim(held, mine, 0, keepdims=False)
        give = lax.dynamic_index_in_dim(held, 1 - mine, 0, keepdims=False)
        held = keep + swapped(give.astype(jnp.bfloat16), axis, bit).astype(jnp.float32)
    return held


def causal_conv(prior_rows, raw_rows, conv_weight, conv_bias):
    joined = jnp.concatenate([prior_rows, raw_rows], axis=0).astype(jnp.float32)
    length = raw_rows.shape[0]
    running = jnp.broadcast_to(conv_bias[None, :], raw_rows.shape)
    for offset in range(conv_weight.shape[0]):
        running = running + conv_weight[offset][None, :] * joined[offset : offset + length]
    return jax.nn.silu(running).astype(jnp.bfloat16)


def body(
    hidden,
    in_weight,
    step_weight,
    group_weight,
    conv_inner,
    inner_bias,
    conv_group,
    group_bias,
    step_bias,
    log_rate,
    skip_weight,
    norm_gain,
    out_weight,
):
    tp_size = lax.axis_size("tp")
    tp_bits = [1 << k for k in range(tp_size.bit_length() - 1)]
    heads_dev = log_rate.shape[0]
    inner_dev = in_weight.shape[2]
    group_cols = 2 * STATE
    per_group_dev = (HEADS // GROUPS) // heads_dev
    group_index = lax.axis_index("tp") // per_group_dev
    zx_weight = in_weight.reshape(in_weight.shape[0], 2 * inner_dev)
    stacked = gather_rows(hidden, "tp", tp_bits)
    levels = len(tp_bits)
    length = tp_size * hidden.shape[0]
    flipped = tuple(reversed(range(levels)))

    def in_order(rows):
        rows = jnp.transpose(rows, flipped + tuple(range(levels, rows.ndim)))
        return rows.reshape((length,) + rows.shape[levels + 1 :])

    projected = jnp.concatenate(
        [
            in_order(jnp.einsum("...d,dn->...n", stacked, zx_weight, preferred_element_type=jnp.float32)),
            in_order(jnp.einsum("...d,dn->...n", stacked, step_weight, preferred_element_type=jnp.float32)),
        ],
        axis=1,
    ).astype(jnp.bfloat16)
    gate_raw = projected[:, :inner_dev]
    inner_raw = projected[:, inner_dev : 2 * inner_dev]
    step_raw = projected[:, 2 * inner_dev :]
    border_rows = KERNEL - 1
    last_rows = stacked[(1,) * levels][hidden.shape[0] - border_rows :]
    before = shifted(last_rows, "ctx", 1)
    inner_prior = jnp.dot(
        before, zx_weight[:, inner_dev:], preferred_element_type=jnp.float32
    ).astype(jnp.bfloat16)
    own_maps = jnp.einsum(
        "...d,sgd->...gs", stacked, group_weight, preferred_element_type=jnp.float32
    ).astype(jnp.bfloat16)
    own_maps = jnp.moveaxis(in_order(own_maps), 1, 0)
    border_maps = jnp.einsum(
        "td,sgd->gts", before, group_weight, preferred_element_type=jnp.float32
    ).astype(jnp.bfloat16)
    own_maps = jnp.concatenate([border_maps, own_maps], axis=1)
    own_maps = jnp.broadcast_to(own_maps[:, None], (GROUPS, per_group_dev) + own_maps.shape[1:])
    own_maps = own_maps.reshape((tp_size,) + own_maps.shape[2:])
    got_maps = lax.all_to_all(own_maps, "tp", 0, 0, tiled=True)
    all_maps = jnp.transpose(got_maps, (1, 0, 2)).reshape(border_rows + length, group_cols)
    map_prior = all_maps[:border_rows]
    map_part = all_maps[border_rows:]
    x_conv = causal_conv(inner_prior, inner_raw, conv_inner, inner_bias)
    own_taps = lax.dynamic_slice_in_dim(conv_group, group_index * group_cols, group_cols, 1)
    own_bias = lax.dynamic_slice_in_dim(group_bias, group_index * group_cols, group_cols, 0)
    maps = causal_conv(map_prior, map_part, own_taps, own_bias)
    step_size = jax.nn.softplus(step_raw.astype(jnp.float32) + step_bias[None, :])
    decay_rate = -jnp.exp(log_rate)
    blocks = length // BLOCK
    x_blocks = x_conv.reshape(blocks, BLOCK, heads_dev, HEAD_DIM)
    input_map = maps[:, :STATE].reshape(blocks, BLOCK, STATE)
    output_map = maps[:, STATE:].reshape(blocks, BLOCK, STATE)
    step_blocks = jnp.swapaxes(step_size.reshape(blocks, BLOCK, heads_dev), 1, 2)
    cumulative = jnp.cumsum(step_blocks * decay_rate[None, :, None], axis=2)
    scores = jnp.einsum("kin,kjn->kij", output_map, input_map, preferred_element_type=jnp.float32)
    causal = jnp.arange(BLOCK)[:, None] >= jnp.arange(BLOCK)[None, :]
    exponent = jnp.where(causal, cumulative[..., :, None] - cumulative[..., None, :], -jnp.inf)
    mixing = (scores[:, None] * jnp.exp(exponent) * step_blocks[..., None, :]).astype(jnp.bfloat16)
    within = jnp.einsum("khij,kjhp->kihp", mixing, x_blocks, preferred_element_type=jnp.float32)
    weight = jnp.exp(cumulative[..., BLOCK - 1 :] - cumulative) * step_blocks
    x_float = x_blocks.astype(jnp.float32)
    weighted = (x_float * jnp.swapaxes(weight, 1, 2)[..., None]).astype(jnp.bfloat16)
    block_state = jnp.einsum(
        "kjhp,kjn->khpn", weighted, input_map, preferred_element_type=jnp.float32
    )
    block_decay = jnp.exp(cumulative[..., BLOCK - 1])

    def advance(carry, item):
        running, product = carry
        block_stop_index, state_here = item
        return (
            (block_stop_index[:, None, None] * running + state_here, product * block_stop_index),
            (running, product),
        )

    empty_state = jnp.zeros((heads_dev, HEAD_DIM, STATE), jnp.float32)
    (dev_state, dev_decay), (local_starts, prefixes) = lax.scan(
        advance, (empty_state, jnp.ones((heads_dev,), jnp.float32)), (block_decay, block_state)
    )
    ctx_size = lax.axis_size("ctx")
    place = lax.axis_index("ctx")
    in_decay = jnp.ones_like(dev_decay)
    in_state = jnp.zeros_like(dev_state)
    run_decay = dev_decay
    run_state = dev_state
    reach = 1
    while reach < ctx_size:
        packed = jnp.concatenate(
            [run_state, jnp.broadcast_to(run_decay[:, None, None], (heads_dev, 1, STATE))], axis=1
        )
        got = shifted(packed.astype(jnp.bfloat16), "ctx", reach).astype(jnp.float32)
        valid = place >= reach
        got_state = jnp.where(valid, got[:, :HEAD_DIM], 0.0)
        got_decay = jnp.where(valid, got[:, HEAD_DIM, 0], 1.0)
        in_state = in_decay[:, None, None] * got_state + in_state
        in_decay = got_decay * in_decay
        run_state = run_decay[:, None, None] * got_state + run_state
        run_decay = got_decay * run_decay
        reach *= 2
    incoming = in_state
    starting = local_starts + prefixes[:, :, None, None] * incoming[None]
    carried = jnp.einsum(
        "kin,khpn->kihp",
        output_map,
        starting.astype(jnp.bfloat16),
        preferred_element_type=jnp.float32,
    )
    carried = carried * jnp.swapaxes(jnp.exp(cumulative), 1, 2)[..., None]
    result_heads = within + carried + skip_weight[None, None, :, None] * x_float
    result_heads = result_heads.reshape(length, inner_dev)
    gated = result_heads * jax.nn.silu(gate_raw.astype(jnp.float32))
    scaled = jnp.concatenate(
        [(gated * norm_gain[None, :]).astype(jnp.bfloat16), (gated * gated).astype(jnp.bfloat16)], axis=1
    )
    width = out_weight.shape[1]
    extended = jnp.concatenate(
        [
            jnp.concatenate([out_weight, jnp.zeros((inner_dev, 128), out_weight.dtype)], axis=1),
            jnp.concatenate(
                [jnp.zeros((inner_dev, width), out_weight.dtype), jnp.ones((inner_dev, 128), out_weight.dtype)],
                axis=1,
            ),
        ],
        axis=0,
    )
    scaled = scaled.reshape((2,) * levels + (length // tp_size, 2 * inner_dev))
    scaled = jnp.transpose(scaled, flipped + (levels, levels + 1))
    partial = jnp.einsum("...c,cn->...n", scaled, extended, preferred_element_type=jnp.float32)
    within_bits = [bit for bit in tp_bits if bit < per_group_dev]
    across_bits = [bit for bit in tp_bits if bit >= per_group_dev]
    held = halve(partial, "tp", within_bits)
    inverse = lax.rsqrt(held[..., width] / (HEADS * HEAD_DIM // GROUPS) + 1e-05)
    held = held[..., :width] * inverse[..., None]
    held = halve(held, "tp", across_bits)
    mixed = held
    return mixed.astype(jnp.bfloat16)


def solution(mesh):
    placed = (
        P(("ctx", "tp"), None),
        P(None, None, "tp"),
        P(None, "tp"),
        P("tp", None, None),
        P(None, "tp"),
        P("tp"),
        P(),
        P(),
        P("tp"),
        P("tp"),
        P("tp"),
        P("tp"),
        P("tp", None),
    )
    return jax.shard_map(
        body, mesh=mesh, in_specs=placed, out_specs=P(("ctx", "tp"), None), check_vma=False
    )
```

```python
import jax
import jax.numpy as jnp
from jax import lax
from jax.sharding import PartitionSpec as P

HEADS = 64
HEAD_DIM = 64
STATE = 128
GROUPS = 4
BLOCK = 256
KERNEL = 4


def shifted(x, axis, by):
    peers = lax.axis_size(axis)
    pairs = [(i, i + by) for i in range(peers) if 0 <= i + by < peers]
    return lax.ppermute(x, axis, pairs)


def swapped(x, axis, bit):
    peers = lax.axis_size(axis)
    return lax.ppermute(x, axis, [(i, i ^ bit) for i in range(peers)])


def gather_rows(rows, axis, bits):
    place = lax.axis_index(axis)
    peers = lax.axis_size(axis)
    held = rows
    for bit in reversed(bits):
        other = swapped(held, axis, bit)
        low = (place & bit) == 0
        held = jnp.where(low, jnp.stack([held, other]), jnp.stack([other, held]))
    return held


def halve(held, axis, bits):
    place = lax.axis_index(axis)
    for bit in bits:
        mine = (place // bit) % 2
        keep = lax.dynamic_index_in_dim(held, mine, 0, keepdims=False)
        give = lax.dynamic_index_in_dim(held, 1 - mine, 0, keepdims=False)
        held = keep + swapped(give.astype(jnp.bfloat16), axis, bit).astype(jnp.float32)
    return held


def causal_conv(prior_rows, raw_rows, conv_weight, conv_bias):
    joined = jnp.concatenate([prior_rows, raw_rows], axis=0).astype(jnp.float32)
    length = raw_rows.shape[0]
    running = jnp.broadcast_to(conv_bias[None, :], raw_rows.shape)
    for offset in range(conv_weight.shape[0]):
        running = running + conv_weight[offset][None, :] * joined[offset : offset + length]
    return jax.nn.silu(running).astype(jnp.bfloat16)


def body(
    hidden,
    in_weight,
    step_weight,
    group_weight,
    conv_inner,
    inner_bias,
    conv_group,
    group_bias,
    step_bias,
    log_rate,
    skip_weight,
    norm_gain,
    out_weight,
):
    tp_size = lax.axis_size("tp")
    tp_bits = [1 << k for k in range(tp_size.bit_length() - 1)]
    heads_dev = log_rate.shape[0]
    inner_dev = in_weight.shape[2]
    group_cols = 2 * STATE
    per_group_dev = (HEADS // GROUPS) // heads_dev
    group_index = lax.axis_index("tp") // per_group_dev
    zx_weight = in_weight.reshape(in_weight.shape[0], 2 * inner_dev)
    stacked = gather_rows(hidden, "tp", tp_bits)
    levels = len(tp_bits)
    length = tp_size * hidden.shape[0]
    flipped = tuple(reversed(range(levels)))

    def in_order(rows):
        rows = jnp.transpose(rows, flipped + tuple(range(levels, rows.ndim)))
        return rows.reshape((length,) + rows.shape[levels + 1 :])

    map_cols = jnp.transpose(group_weight, (2, 1, 0)).reshape(group_weight.shape[2], -1)
    joined = jnp.concatenate([zx_weight, step_weight, map_cols], axis=1)
    projected = in_order(
        jnp.einsum("...d,dn->...n", stacked, joined, preferred_element_type=jnp.float32)
    ).astype(jnp.bfloat16)
    gate_raw = projected[:, :inner_dev]
    inner_raw = projected[:, inner_dev : 2 * inner_dev]
    step_raw = projected[:, 2 * inner_dev : 2 * inner_dev + heads_dev]
    own_maps = projected[:, 2 * inner_dev + heads_dev :].reshape(length, GROUPS, -1)
    own_maps = jnp.moveaxis(own_maps, 1, 0)
    own_maps = jnp.broadcast_to(own_maps[:, None], (GROUPS, per_group_dev) + own_maps.shape[1:])
    own_maps = own_maps.reshape((tp_size,) + own_maps.shape[2:])
    got_maps = lax.all_to_all(own_maps, "tp", 0, 0, tiled=True)
    map_part = jnp.transpose(got_maps, (1, 0, 2)).reshape(length, group_cols)
    border_rows = KERNEL - 1
    prior = shifted(
        jnp.concatenate([inner_raw[length - border_rows :], map_part[length - border_rows :]], axis=1),
        "ctx",
        1,
    )
    inner_prior = prior[:, :inner_dev]
    map_prior = prior[:, inner_dev:]
    x_conv = causal_conv(inner_prior, inner_raw, conv_inner, inner_bias)
    own_taps = lax.dynamic_slice_in_dim(conv_group, group_index * group_cols, group_cols, 1)
    own_bias = lax.dynamic_slice_in_dim(group_bias, group_index * group_cols, group_cols, 0)
    maps = causal_conv(map_prior, map_part, own_taps, own_bias)
    step_size = jax.nn.softplus(step_raw.astype(jnp.float32) + step_bias[None, :])
    decay_rate = -jnp.exp(log_rate)
    blocks = length // BLOCK
    x_blocks = x_conv.reshape(blocks, BLOCK, heads_dev, HEAD_DIM)
    input_map = maps[:, :STATE].reshape(blocks, BLOCK, STATE)
    output_map = maps[:, STATE:].reshape(blocks, BLOCK, STATE)
    step_blocks = jnp.swapaxes(step_size.reshape(blocks, BLOCK, heads_dev), 1, 2)
    cumulative = jnp.cumsum(step_blocks * decay_rate[None, :, None], axis=2)
    scores = jnp.einsum("kin,kjn->kij", output_map, input_map, preferred_element_type=jnp.float32)
    causal = jnp.arange(BLOCK)[:, None] >= jnp.arange(BLOCK)[None, :]
    exponent = jnp.where(causal, cumulative[..., :, None] - cumulative[..., None, :], -jnp.inf)
    mixing = (scores[:, None] * jnp.exp(exponent) * step_blocks[..., None, :]).astype(jnp.bfloat16)
    within = jnp.einsum("khij,kjhp->kihp", mixing, x_blocks, preferred_element_type=jnp.float32)
    weight = jnp.exp(cumulative[..., BLOCK - 1 :] - cumulative) * step_blocks
    x_float = x_blocks.astype(jnp.float32)
    weighted = (x_float * jnp.swapaxes(weight, 1, 2)[..., None]).astype(jnp.bfloat16)
    block_state = jnp.einsum(
        "kjhp,kjn->khpn", weighted, input_map, preferred_element_type=jnp.float32
    )
    block_decay = jnp.exp(cumulative[..., BLOCK - 1])

    def advance(carry, item):
        running, product = carry
        block_stop_index, state_here = item
        return (
            (block_stop_index[:, None, None] * running + state_here, product * block_stop_index),
            (running, product),
        )

    empty_state = jnp.zeros((heads_dev, HEAD_DIM, STATE), jnp.float32)
    (dev_state, dev_decay), (local_starts, prefixes) = lax.scan(
        advance, (empty_state, jnp.ones((heads_dev,), jnp.float32)), (block_decay, block_state)
    )
    ctx_size = lax.axis_size("ctx")
    place = lax.axis_index("ctx")
    in_decay = jnp.ones_like(dev_decay)
    in_state = jnp.zeros_like(dev_state)
    run_decay = dev_decay
    run_state = dev_state
    reach = 1
    while reach < ctx_size:
        packed = jnp.concatenate(
            [run_state, jnp.broadcast_to(run_decay[:, None, None], (heads_dev, 1, STATE))], axis=1
        )
        got = shifted(packed.astype(jnp.bfloat16), "ctx", reach).astype(jnp.float32)
        valid = place >= reach
        got_state = jnp.where(valid, got[:, :HEAD_DIM], 0.0)
        got_decay = jnp.where(valid, got[:, HEAD_DIM, 0], 1.0)
        in_state = in_decay[:, None, None] * got_state + in_state
        in_decay = got_decay * in_decay
        run_state = run_decay[:, None, None] * got_state + run_state
        run_decay = got_decay * run_decay
        reach *= 2
    incoming = in_state
    starting = local_starts + prefixes[:, :, None, None] * incoming[None]
    carried = jnp.einsum(
        "kin,khpn->kihp",
        output_map,
        starting.astype(jnp.bfloat16),
        preferred_element_type=jnp.float32,
    )
    carried = carried * jnp.swapaxes(jnp.exp(cumulative), 1, 2)[..., None]
    result_heads = within + carried + skip_weight[None, None, :, None] * x_float
    result_heads = result_heads.reshape(length, inner_dev)
    gated = result_heads * jax.nn.silu(gate_raw.astype(jnp.float32))
    scaled = jnp.concatenate(
        [(gated * norm_gain[None, :]).astype(jnp.bfloat16), (gated * gated).astype(jnp.bfloat16)], axis=1
    )
    width = out_weight.shape[1]
    extended = jnp.concatenate(
        [
            jnp.concatenate([out_weight, jnp.zeros((inner_dev, 128), out_weight.dtype)], axis=1),
            jnp.concatenate(
                [jnp.zeros((inner_dev, width), out_weight.dtype), jnp.ones((inner_dev, 128), out_weight.dtype)],
                axis=1,
            ),
        ],
        axis=0,
    )
    scaled = scaled.reshape((2,) * levels + (length // tp_size, 2 * inner_dev))
    scaled = jnp.transpose(scaled, flipped + (levels, levels + 1))
    partial = jnp.einsum("...c,cn->...n", scaled, extended, preferred_element_type=jnp.float32)
    within_bits = [bit for bit in tp_bits if bit < per_group_dev]
    across_bits = [bit for bit in tp_bits if bit >= per_group_dev]
    held = halve(partial, "tp", within_bits)
    inverse = lax.rsqrt(held[..., width] / (HEADS * HEAD_DIM // GROUPS) + 1e-05)
    held = held[..., :width] * inverse[..., None]
    held = halve(held, "tp", across_bits)
    mixed = held
    return mixed.astype(jnp.bfloat16)


def solution(mesh):
    placed = (
        P(("ctx", "tp"), None),
        P(None, None, "tp"),
        P(None, "tp"),
        P("tp", None, None),
        P(None, "tp"),
        P("tp"),
        P(),
        P(),
        P("tp"),
        P("tp"),
        P("tp"),
        P("tp"),
        P("tp", None),
    )
    return jax.shard_map(
        body, mesh=mesh, in_specs=placed, out_specs=P(("ctx", "tp"), None), check_vma=False
    )
```

```python
import jax
import jax.numpy as jnp
from jax import lax
from jax.sharding import Mesh, PartitionSpec as P

HEADS = 64
HEAD_DIM = 64
STATE = 128
GROUPS = 4
BLOCK = 256
KERNEL = 4


def shifted(x, axis, by):
    peers = lax.axis_size(axis)
    pairs = [(i, i + by) for i in range(peers) if 0 <= i + by < peers]
    return lax.ppermute(x, axis, pairs)


def swapped(x, axis, bit):
    peers = lax.axis_size(axis)
    return lax.ppermute(x, axis, [(i, i ^ bit) for i in range(peers)])


def gather_rows(rows, axis, bits):
    place = lax.axis_index(axis)
    peers = lax.axis_size(axis)
    held = rows
    for bit in reversed(bits):
        other = swapped(held, axis, bit)
        low = (place & bit) == 0
        held = jnp.where(low, jnp.stack([held, other]), jnp.stack([other, held]))
    return held


def halve(held, axis, bits):
    place = lax.axis_index(axis)
    for bit in bits:
        mine = (place // bit) % 2
        keep = lax.dynamic_index_in_dim(held, mine, 0, keepdims=False)
        give = lax.dynamic_index_in_dim(held, 1 - mine, 0, keepdims=False)
        held = keep + swapped(give.astype(jnp.bfloat16), axis, bit).astype(jnp.float32)
    return held


def causal_conv(prior_rows, raw_rows, conv_weight, conv_bias):
    joined = jnp.concatenate([prior_rows, raw_rows], axis=0).astype(jnp.float32)
    length = raw_rows.shape[0]
    running = jnp.broadcast_to(conv_bias[None, :], raw_rows.shape)
    for offset in range(conv_weight.shape[0]):
        running = running + conv_weight[offset][None, :] * joined[offset : offset + length]
    return jax.nn.silu(running).astype(jnp.bfloat16)


def body(
    hidden,
    in_weight,
    step_weight,
    group_weight,
    conv_inner,
    inner_bias,
    conv_group,
    group_bias,
    step_bias,
    log_rate,
    skip_weight,
    norm_gain,
    out_weight,
):
    tp_size = lax.axis_size("tp")
    tp_bits = [1 << k for k in range(tp_size.bit_length() - 1)]
    heads_dev = log_rate.shape[0]
    inner_dev = in_weight.shape[2]
    group_cols = 2 * STATE
    per_group_dev = (HEADS // GROUPS) // heads_dev
    group_index = lax.axis_index("tp") // per_group_dev
    zx_weight = in_weight.reshape(in_weight.shape[0], 2 * inner_dev)
    stacked = gather_rows(hidden, "tp", tp_bits)
    levels = len(tp_bits)
    length = tp_size * hidden.shape[0]
    flipped = tuple(reversed(range(levels)))

    def in_order(rows):
        rows = jnp.transpose(rows, flipped + tuple(range(levels, rows.ndim)))
        return rows.reshape((length,) + rows.shape[levels + 1 :])

    map_cols = jnp.transpose(group_weight, (2, 1, 0)).reshape(group_weight.shape[2], -1)
    joined = jnp.concatenate([zx_weight, step_weight, map_cols], axis=1)
    projected = in_order(
        jnp.einsum("...d,dn->...n", stacked, joined, preferred_element_type=jnp.float32)
    ).astype(jnp.bfloat16)
    gate_raw = projected[:, :inner_dev]
    inner_raw = projected[:, inner_dev : 2 * inner_dev]
    step_raw = projected[:, 2 * inner_dev : 2 * inner_dev + heads_dev]
    own_maps = projected[:, 2 * inner_dev + heads_dev :].reshape(length, GROUPS, -1)
    own_maps = jnp.moveaxis(own_maps, 1, 0)
    own_maps = jnp.broadcast_to(own_maps[:, None], (GROUPS, per_group_dev) + own_maps.shape[1:])
    own_maps = own_maps.reshape((tp_size,) + own_maps.shape[2:])
    got_maps = lax.all_to_all(own_maps, "tp", 0, 0, tiled=True)
    map_part = jnp.transpose(got_maps, (1, 0, 2)).reshape(length, group_cols)
    border_rows = KERNEL - 1
    prior = shifted(
        jnp.concatenate([inner_raw[length - border_rows :], map_part[length - border_rows :]], axis=1),
        ("z", "x"),
        1,
    )
    inner_prior = prior[:, :inner_dev]
    map_prior = prior[:, inner_dev:]
    x_conv = causal_conv(inner_prior, inner_raw, conv_inner, inner_bias)
    own_taps = lax.dynamic_slice_in_dim(conv_group, group_index * group_cols, group_cols, 1)
    own_bias = lax.dynamic_slice_in_dim(group_bias, group_index * group_cols, group_cols, 0)
    maps = causal_conv(map_prior, map_part, own_taps, own_bias)
    step_size = jax.nn.softplus(step_raw.astype(jnp.float32) + step_bias[None, :])
    decay_rate = -jnp.exp(log_rate)
    blocks = length // BLOCK
    x_blocks = x_conv.reshape(blocks, BLOCK, heads_dev, HEAD_DIM)
    input_map = maps[:, :STATE].reshape(blocks, BLOCK, STATE)
    output_map = maps[:, STATE:].reshape(blocks, BLOCK, STATE)
    step_blocks = jnp.swapaxes(step_size.reshape(blocks, BLOCK, heads_dev), 1, 2)
    cumulative = jnp.cumsum(step_blocks * decay_rate[None, :, None], axis=2)
    scores = jnp.einsum("kin,kjn->kij", output_map, input_map, preferred_element_type=jnp.float32)
    causal = jnp.arange(BLOCK)[:, None] >= jnp.arange(BLOCK)[None, :]
    exponent = jnp.where(causal, cumulative[..., :, None] - cumulative[..., None, :], -jnp.inf)
    mixing = (scores[:, None] * jnp.exp(exponent) * step_blocks[..., None, :]).astype(jnp.bfloat16)
    within = jnp.einsum("khij,kjhp->kihp", mixing, x_blocks, preferred_element_type=jnp.float32)
    weight = jnp.exp(cumulative[..., BLOCK - 1 :] - cumulative) * step_blocks
    x_float = x_blocks.astype(jnp.float32)
    weighted = (x_float * jnp.swapaxes(weight, 1, 2)[..., None]).astype(jnp.bfloat16)
    block_state = jnp.einsum(
        "kjhp,kjn->khpn", weighted, input_map, preferred_element_type=jnp.float32
    )
    block_decay = jnp.exp(cumulative[..., BLOCK - 1])

    def advance(carry, item):
        running, product = carry
        block_stop_index, state_here = item
        return (
            (block_stop_index[:, None, None] * running + state_here, product * block_stop_index),
            (running, product),
        )

    empty_state = jnp.zeros((heads_dev, HEAD_DIM, STATE), jnp.float32)
    (dev_state, dev_decay), (local_starts, prefixes) = lax.scan(
        advance, (empty_state, jnp.ones((heads_dev,), jnp.float32)), (block_decay, block_state)
    )
    x_peers = lax.axis_size("x")
    x_place = lax.axis_index("x")
    packed = jnp.concatenate(
        [dev_state, jnp.broadcast_to(dev_decay[:, None, None], (heads_dev, 1, STATE))], axis=1
    ).astype(jnp.bfloat16)
    row = lax.all_to_all(
        jnp.broadcast_to(packed[None], (x_peers,) + packed.shape), "x", 0, 0, tiled=True
    ).astype(jnp.float32)
    row_decay = jnp.ones_like(dev_decay)
    row_state = jnp.zeros_like(dev_state)
    in_decay = jnp.ones_like(dev_decay)
    in_state = jnp.zeros_like(dev_state)
    for k in reversed(range(x_peers)):
        got_state = row[k, :, :HEAD_DIM]
        got_decay = row[k, :, HEAD_DIM, 0]
        earlier = k < x_place
        in_state = jnp.where(earlier, in_decay[:, None, None] * got_state + in_state, in_state)
        in_decay = jnp.where(earlier, got_decay * in_decay, in_decay)
        row_state = row_decay[:, None, None] * got_state + row_state
        row_decay = got_decay * row_decay
    z_peers = lax.axis_size("z")
    z_place = lax.axis_index("z")
    pre_decay = jnp.ones_like(dev_decay)
    pre_state = jnp.zeros_like(dev_state)
    run_decay = row_decay
    run_state = row_state
    reach = 1
    while reach < z_peers:
        packed = jnp.concatenate(
            [run_state, jnp.broadcast_to(run_decay[:, None, None], (heads_dev, 1, STATE))], axis=1
        )
        got = shifted(packed.astype(jnp.bfloat16), "z", reach).astype(jnp.float32)
        valid = z_place >= reach
        got_state = jnp.where(valid, got[:, :HEAD_DIM], 0.0)
        got_decay = jnp.where(valid, got[:, HEAD_DIM, 0], 1.0)
        pre_state = pre_decay[:, None, None] * got_state + pre_state
        pre_decay = got_decay * pre_decay
        run_state = run_decay[:, None, None] * got_state + run_state
        run_decay = got_decay * run_decay
        reach *= 2
    in_state = in_decay[:, None, None] * pre_state + in_state
    incoming = in_state
    starting = local_starts + prefixes[:, :, None, None] * incoming[None]
    carried = jnp.einsum(
        "kin,khpn->kihp",
        output_map,
        starting.astype(jnp.bfloat16),
        preferred_element_type=jnp.float32,
    )
    carried = carried * jnp.swapaxes(jnp.exp(cumulative), 1, 2)[..., None]
    result_heads = within + carried + skip_weight[None, None, :, None] * x_float
    result_heads = result_heads.reshape(length, inner_dev)
    gated = result_heads * jax.nn.silu(gate_raw.astype(jnp.float32))
    scaled = jnp.concatenate(
        [(gated * norm_gain[None, :]).astype(jnp.bfloat16), (gated * gated).astype(jnp.bfloat16)], axis=1
    )
    width = out_weight.shape[1]
    extended = jnp.concatenate(
        [
            jnp.concatenate([out_weight, jnp.zeros((inner_dev, 128), out_weight.dtype)], axis=1),
            jnp.concatenate(
                [jnp.zeros((inner_dev, width), out_weight.dtype), jnp.ones((inner_dev, 128), out_weight.dtype)],
                axis=1,
            ),
        ],
        axis=0,
    )
    scaled = scaled.reshape((2,) * levels + (length // tp_size, 2 * inner_dev))
    scaled = jnp.transpose(scaled, flipped + (levels, levels + 1))
    partial = jnp.einsum("...c,cn->...n", scaled, extended, preferred_element_type=jnp.float32)
    within_bits = [bit for bit in tp_bits if bit < per_group_dev]
    across_bits = [bit for bit in tp_bits if bit >= per_group_dev]
    held = halve(partial, "tp", within_bits)
    inverse = lax.rsqrt(held[..., width] / (HEADS * HEAD_DIM // GROUPS) + 1e-05)
    held = held[..., :width] * inverse[..., None]
    held = halve(held, "tp", across_bits)
    mixed = held
    return mixed.astype(jnp.bfloat16)


def solution(mesh):
    ctx_size = mesh.shape["ctx"]
    x_size = 4 if ctx_size % 4 == 0 else ctx_size
    fine = Mesh(
        mesh.devices.reshape(ctx_size // x_size, x_size, mesh.shape["tp"]), ("z", "x", "tp")
    )
    rows = ("z", "x", "tp")
    placed = (
        P(rows, None),
        P(None, None, "tp"),
        P(None, "tp"),
        P("tp", None, None),
        P(None, "tp"),
        P("tp"),
        P(),
        P(),
        P("tp"),
        P("tp"),
        P("tp"),
        P("tp"),
        P("tp", None),
    )
    return jax.shard_map(body, mesh=fine, in_specs=placed, out_specs=P(rows, None), check_vma=False)
```

```python
import jax
import jax.numpy as jnp
from jax import lax
from jax.sharding import Mesh, PartitionSpec as P

HEADS = 64
HEAD_DIM = 64
STATE = 128
GROUPS = 4
BLOCK = 256
KERNEL = 4


def shifted(x, axis, by):
    peers = lax.axis_size(axis)
    pairs = [(i, i + by) for i in range(peers) if 0 <= i + by < peers]
    return lax.ppermute(x, axis, pairs)


def swapped(x, axis, bit):
    peers = lax.axis_size(axis)
    return lax.ppermute(x, axis, [(i, i ^ bit) for i in range(peers)])


def gather_rows(rows, axis, bits):
    place = lax.axis_index(axis)
    peers = lax.axis_size(axis)
    held = rows
    for bit in reversed(bits):
        other = swapped(held, axis, bit)
        low = (place & bit) == 0
        held = jnp.where(low, jnp.stack([held, other]), jnp.stack([other, held]))
    return held


def halve(held, axis, bits):
    place = lax.axis_index(axis)
    for bit in bits:
        mine = (place // bit) % 2
        keep = lax.dynamic_index_in_dim(held, mine, 0, keepdims=False)
        give = lax.dynamic_index_in_dim(held, 1 - mine, 0, keepdims=False)
        held = keep + swapped(give.astype(jnp.bfloat16), axis, bit).astype(jnp.float32)
    return held


def causal_conv(prior_rows, raw_rows, conv_weight, conv_bias):
    joined = jnp.concatenate([prior_rows, raw_rows], axis=0).astype(jnp.float32)
    length = raw_rows.shape[0]
    running = jnp.broadcast_to(conv_bias[None, :], raw_rows.shape)
    for offset in range(conv_weight.shape[0]):
        running = running + conv_weight[offset][None, :] * joined[offset : offset + length]
    return jax.nn.silu(running).astype(jnp.bfloat16)


def body(
    hidden,
    in_weight,
    step_weight,
    group_weight,
    conv_inner,
    inner_bias,
    conv_group,
    group_bias,
    step_bias,
    log_rate,
    skip_weight,
    norm_gain,
    out_weight,
):
    tp_size = lax.axis_size(TP_AXES)
    heads_dev = log_rate.shape[0]
    inner_dev = in_weight.shape[2]
    group_cols = 2 * STATE
    per_group_dev = (HEADS // GROUPS) // heads_dev
    group_index = lax.axis_index("tg")
    zx_weight = in_weight.reshape(in_weight.shape[0], 2 * inner_dev)
    ring = ("tg", "yl")
    ring_size = lax.axis_size(ring)
    length = tp_size * hidden.shape[0]
    ring_rows = lax.all_to_all(
        jnp.broadcast_to(hidden[None], (ring_size,) + hidden.shape), ring, 0, 0, tiled=True
    )
    other_rows = lax.ppermute(ring_rows, "tc", [(0, 1), (1, 0)])
    first = lax.axis_index("tc") == 0
    stacked = jnp.where(
        first, jnp.stack([ring_rows, other_rows], axis=1), jnp.stack([other_rows, ring_rows], axis=1)
    ).reshape((length,) + hidden.shape[1:])

    def in_order(rows):
        return rows

    map_cols = jnp.transpose(group_weight, (2, 1, 0)).reshape(group_weight.shape[2], -1)
    joined = jnp.concatenate([zx_weight, step_weight, map_cols], axis=1)
    projected = in_order(
        jnp.einsum("...d,dn->...n", stacked, joined, preferred_element_type=jnp.float32)
    ).astype(jnp.bfloat16)
    gate_raw = projected[:, :inner_dev]
    inner_raw = projected[:, inner_dev : 2 * inner_dev]
    step_raw = projected[:, 2 * inner_dev : 2 * inner_dev + heads_dev]
    own_maps = projected[:, 2 * inner_dev + heads_dev :].reshape(length, GROUPS, -1)
    own_maps = jnp.moveaxis(own_maps, 1, 0)
    own_maps = jnp.broadcast_to(own_maps[:, None], (GROUPS, per_group_dev) + own_maps.shape[1:])
    own_maps = own_maps.reshape((tp_size,) + own_maps.shape[2:])
    got_maps = lax.all_to_all(own_maps, TP_AXES, 0, 0, tiled=True)
    map_part = jnp.transpose(got_maps, (1, 0, 2)).reshape(length, group_cols)
    border_rows = KERNEL - 1
    prior = shifted(
        jnp.concatenate([inner_raw[length - border_rows :], map_part[length - border_rows :]], axis=1),
        ("z", "x"),
        1,
    )
    inner_prior = prior[:, :inner_dev]
    map_prior = prior[:, inner_dev:]
    x_conv = causal_conv(inner_prior, inner_raw, conv_inner, inner_bias)
    own_taps = lax.dynamic_slice_in_dim(conv_group, group_index * group_cols, group_cols, 1)
    own_bias = lax.dynamic_slice_in_dim(group_bias, group_index * group_cols, group_cols, 0)
    maps = causal_conv(map_prior, map_part, own_taps, own_bias)
    step_size = jax.nn.softplus(step_raw.astype(jnp.float32) + step_bias[None, :])
    decay_rate = -jnp.exp(log_rate)
    blocks = length // BLOCK
    x_blocks = x_conv.reshape(blocks, BLOCK, heads_dev, HEAD_DIM)
    input_map = maps[:, :STATE].reshape(blocks, BLOCK, STATE)
    output_map = maps[:, STATE:].reshape(blocks, BLOCK, STATE)
    step_blocks = jnp.swapaxes(step_size.reshape(blocks, BLOCK, heads_dev), 1, 2)
    cumulative = jnp.cumsum(step_blocks * decay_rate[None, :, None], axis=2)
    scores = jnp.einsum("kin,kjn->kij", output_map, input_map, preferred_element_type=jnp.float32)
    causal = jnp.arange(BLOCK)[:, None] >= jnp.arange(BLOCK)[None, :]
    exponent = jnp.where(causal, cumulative[..., :, None] - cumulative[..., None, :], -jnp.inf)
    mixing = (scores[:, None] * jnp.exp(exponent) * step_blocks[..., None, :]).astype(jnp.bfloat16)
    within = jnp.einsum("khij,kjhp->kihp", mixing, x_blocks, preferred_element_type=jnp.float32)
    weight = jnp.exp(cumulative[..., BLOCK - 1 :] - cumulative) * step_blocks
    x_float = x_blocks.astype(jnp.float32)
    weighted = (x_float * jnp.swapaxes(weight, 1, 2)[..., None]).astype(jnp.bfloat16)
    block_state = jnp.einsum(
        "kjhp,kjn->khpn", weighted, input_map, preferred_element_type=jnp.float32
    )
    block_decay = jnp.exp(cumulative[..., BLOCK - 1])

    def advance(carry, item):
        running, product = carry
        block_stop_index, state_here = item
        return (
            (block_stop_index[:, None, None] * running + state_here, product * block_stop_index),
            (running, product),
        )

    empty_state = jnp.zeros((heads_dev, HEAD_DIM, STATE), jnp.float32)
    (dev_state, dev_decay), (local_starts, prefixes) = lax.scan(
        advance, (empty_state, jnp.ones((heads_dev,), jnp.float32)), (block_decay, block_state)
    )
    x_peers = lax.axis_size("x")
    x_place = lax.axis_index("x")
    packed = jnp.concatenate(
        [dev_state, jnp.broadcast_to(dev_decay[:, None, None], (heads_dev, 1, STATE))], axis=1
    ).astype(jnp.bfloat16)
    row = lax.all_to_all(
        jnp.broadcast_to(packed[None], (x_peers,) + packed.shape), "x", 0, 0, tiled=True
    ).astype(jnp.float32)
    row_decay = jnp.ones_like(dev_decay)
    row_state = jnp.zeros_like(dev_state)
    in_decay = jnp.ones_like(dev_decay)
    in_state = jnp.zeros_like(dev_state)
    for k in reversed(range(x_peers)):
        got_state = row[k, :, :HEAD_DIM]
        got_decay = row[k, :, HEAD_DIM, 0]
        earlier = k < x_place
        in_state = jnp.where(earlier, in_decay[:, None, None] * got_state + in_state, in_state)
        in_decay = jnp.where(earlier, got_decay * in_decay, in_decay)
        row_state = row_decay[:, None, None] * got_state + row_state
        row_decay = got_decay * row_decay
    z_peers = lax.axis_size("z")
    z_place = lax.axis_index("z")
    pre_decay = jnp.ones_like(dev_decay)
    pre_state = jnp.zeros_like(dev_state)
    run_decay = row_decay
    run_state = row_state
    reach = 1
    while reach < z_peers:
        packed = jnp.concatenate(
            [run_state, jnp.broadcast_to(run_decay[:, None, None], (heads_dev, 1, STATE))], axis=1
        )
        got = shifted(packed.astype(jnp.bfloat16), "z", reach).astype(jnp.float32)
        valid = z_place >= reach
        got_state = jnp.where(valid, got[:, :HEAD_DIM], 0.0)
        got_decay = jnp.where(valid, got[:, HEAD_DIM, 0], 1.0)
        pre_state = pre_decay[:, None, None] * got_state + pre_state
        pre_decay = got_decay * pre_decay
        run_state = run_decay[:, None, None] * got_state + run_state
        run_decay = got_decay * run_decay
        reach *= 2
    in_state = in_decay[:, None, None] * pre_state + in_state
    incoming = in_state
    starting = local_starts + prefixes[:, :, None, None] * incoming[None]
    carried = jnp.einsum(
        "kin,khpn->kihp",
        output_map,
        starting.astype(jnp.bfloat16),
        preferred_element_type=jnp.float32,
    )
    carried = carried * jnp.swapaxes(jnp.exp(cumulative), 1, 2)[..., None]
    result_heads = within + carried + skip_weight[None, None, :, None] * x_float
    result_heads = result_heads.reshape(length, inner_dev)
    gated = result_heads * jax.nn.silu(gate_raw.astype(jnp.float32))
    scaled = jnp.concatenate(
        [(gated * norm_gain[None, :]).astype(jnp.bfloat16), (gated * gated).astype(jnp.bfloat16)], axis=1
    )
    width = out_weight.shape[1]
    extended = jnp.concatenate(
        [
            jnp.concatenate([out_weight, jnp.zeros((inner_dev, 128), out_weight.dtype)], axis=1),
            jnp.concatenate(
                [jnp.zeros((inner_dev, width), out_weight.dtype), jnp.ones((inner_dev, 128), out_weight.dtype)],
                axis=1,
            ),
        ],
        axis=0,
    )
    groups_here = lax.axis_size("tg")
    per = length // tp_size
    scaled = scaled.reshape((groups_here, 2, 2, per, 2 * inner_dev))
    scaled = jnp.transpose(scaled, (2, 1, 0, 3, 4))
    partial = jnp.einsum("...c,cn->...n", scaled, extended, preferred_element_type=jnp.float32)
    for axis in ("tc", "yl"):
        mine = lax.axis_index(axis)
        keep = lax.dynamic_index_in_dim(partial, mine, 0, keepdims=False)
        give = lax.dynamic_index_in_dim(partial, 1 - mine, 0, keepdims=False)
        partial = keep + lax.ppermute(give.astype(jnp.bfloat16), axis, [(0, 1), (1, 0)]).astype(jnp.float32)
    inverse = lax.rsqrt(partial[..., width] / (HEADS * HEAD_DIM // GROUPS) + 1e-05)
    held = (partial[..., :width] * inverse[..., None]).astype(jnp.bfloat16)
    arrived = lax.all_to_all(held, "tg", 0, 0, tiled=True)
    mixed = jnp.sum(arrived.astype(jnp.float32), axis=0)
    return mixed.astype(jnp.bfloat16)


TP_AXES = ("tg", "yl", "tc")


def solution(mesh):
    ctx_size = mesh.shape["ctx"]
    tp_size = mesh.shape["tp"]
    x_size = 4 if ctx_size % 4 == 0 else ctx_size
    fine = Mesh(
        mesh.devices.reshape(ctx_size // x_size, x_size, tp_size // 4, 2, 2), ("z", "x") + TP_AXES
    )
    rows = ("z", "x") + TP_AXES
    tp = TP_AXES
    placed = (
        P(rows, None),
        P(None, None, tp),
        P(None, tp),
        P(tp, None, None),
        P(None, tp),
        P(tp),
        P(),
        P(),
        P(tp),
        P(tp),
        P(tp),
        P(tp),
        P(tp, None),
    )
    return jax.shard_map(body, mesh=fine, in_specs=placed, out_specs=P(rows, None), check_vma=False)
```

```python
import jax
import jax.numpy as jnp
from jax import lax
from jax.sharding import Mesh, PartitionSpec as P

HEADS = 64
HEAD_DIM = 64
STATE = 128
GROUPS = 4
BLOCK = 256
KERNEL = 4


def shifted(x, axis, by):
    peers = lax.axis_size(axis)
    pairs = [(i, i + by) for i in range(peers) if 0 <= i + by < peers]
    return lax.ppermute(x, axis, pairs)


def swapped(x, axis, bit):
    peers = lax.axis_size(axis)
    return lax.ppermute(x, axis, [(i, i ^ bit) for i in range(peers)])


def gather_rows(rows, axis, bits):
    place = lax.axis_index(axis)
    peers = lax.axis_size(axis)
    held = rows
    for bit in reversed(bits):
        other = swapped(held, axis, bit)
        low = (place & bit) == 0
        held = jnp.where(low, jnp.stack([held, other]), jnp.stack([other, held]))
    return held


def halve(held, axis, bits):
    place = lax.axis_index(axis)
    for bit in bits:
        mine = (place // bit) % 2
        keep = lax.dynamic_index_in_dim(held, mine, 0, keepdims=False)
        give = lax.dynamic_index_in_dim(held, 1 - mine, 0, keepdims=False)
        held = keep + swapped(give.astype(jnp.bfloat16), axis, bit).astype(jnp.float32)
    return held


def causal_conv(prior_rows, raw_rows, conv_weight, conv_bias):
    joined = jnp.concatenate([prior_rows, raw_rows], axis=0).astype(jnp.float32)
    length = raw_rows.shape[0]
    running = jnp.broadcast_to(conv_bias[None, :], raw_rows.shape)
    for offset in range(conv_weight.shape[0]):
        running = running + conv_weight[offset][None, :] * joined[offset : offset + length]
    return jax.nn.silu(running).astype(jnp.bfloat16)


def body(
    hidden,
    in_weight,
    step_weight,
    group_weight,
    conv_inner,
    inner_bias,
    conv_group,
    group_bias,
    step_bias,
    log_rate,
    skip_weight,
    norm_gain,
    out_weight,
):
    tp_size = lax.axis_size(TP_AXES)
    heads_dev = log_rate.shape[0]
    inner_dev = in_weight.shape[2]
    group_cols = 2 * STATE
    per_group_dev = (HEADS // GROUPS) // heads_dev
    group_index = lax.axis_index("tg")
    zx_weight = in_weight.reshape(in_weight.shape[0], 2 * inner_dev)
    ring = ("tg", "yl")
    ring_size = lax.axis_size(ring)
    length = tp_size * hidden.shape[0]
    ring_rows = lax.all_to_all(
        jnp.broadcast_to(hidden[None], (ring_size,) + hidden.shape), ring, 0, 0, tiled=True
    )
    other_rows = lax.ppermute(ring_rows, "tc", [(0, 1), (1, 0)])
    first = lax.axis_index("tc") == 0
    stacked = jnp.where(
        first, jnp.stack([ring_rows, other_rows], axis=1), jnp.stack([other_rows, ring_rows], axis=1)
    ).reshape((length,) + hidden.shape[1:])

    def in_order(rows):
        return rows

    map_cols = jnp.transpose(group_weight, (2, 1, 0)).reshape(group_weight.shape[2], -1)
    joined = jnp.concatenate([zx_weight, step_weight, map_cols], axis=1)
    projected = in_order(
        jnp.einsum("...d,dn->...n", stacked, joined, preferred_element_type=jnp.float32)
    ).astype(jnp.bfloat16)
    gate_raw = projected[:, :inner_dev]
    inner_raw = projected[:, inner_dev : 2 * inner_dev]
    step_raw = projected[:, 2 * inner_dev : 2 * inner_dev + heads_dev]
    own_maps = projected[:, 2 * inner_dev + heads_dev :].reshape(length, GROUPS, -1)
    own_maps = jnp.moveaxis(own_maps, 1, 0)
    own_maps = jnp.broadcast_to(own_maps[:, None], (GROUPS, per_group_dev) + own_maps.shape[1:])
    own_maps = own_maps.reshape((tp_size,) + own_maps.shape[2:])
    got_maps = lax.all_to_all(own_maps, TP_AXES, 0, 0, tiled=True)
    map_part = jnp.transpose(got_maps, (1, 0, 2)).reshape(length, group_cols)
    border_rows = KERNEL - 1
    prior = shifted(
        jnp.concatenate([inner_raw[length - border_rows :], map_part[length - border_rows :]], axis=1),
        ("zh", "zl", "x"),
        1,
    )
    inner_prior = prior[:, :inner_dev]
    map_prior = prior[:, inner_dev:]
    x_conv = causal_conv(inner_prior, inner_raw, conv_inner, inner_bias)
    own_taps = lax.dynamic_slice_in_dim(conv_group, group_index * group_cols, group_cols, 1)
    own_bias = lax.dynamic_slice_in_dim(group_bias, group_index * group_cols, group_cols, 0)
    maps = causal_conv(map_prior, map_part, own_taps, own_bias)
    step_size = jax.nn.softplus(step_raw.astype(jnp.float32) + step_bias[None, :])
    decay_rate = -jnp.exp(log_rate)
    blocks = length // BLOCK
    x_blocks = x_conv.reshape(blocks, BLOCK, heads_dev, HEAD_DIM)
    input_map = maps[:, :STATE].reshape(blocks, BLOCK, STATE)
    output_map = maps[:, STATE:].reshape(blocks, BLOCK, STATE)
    step_blocks = jnp.swapaxes(step_size.reshape(blocks, BLOCK, heads_dev), 1, 2)
    cumulative = jnp.cumsum(step_blocks * decay_rate[None, :, None], axis=2)
    scores = jnp.einsum("kin,kjn->kij", output_map, input_map, preferred_element_type=jnp.float32)
    causal = jnp.arange(BLOCK)[:, None] >= jnp.arange(BLOCK)[None, :]
    exponent = jnp.where(causal, cumulative[..., :, None] - cumulative[..., None, :], -jnp.inf)
    mixing = (scores[:, None] * jnp.exp(exponent) * step_blocks[..., None, :]).astype(jnp.bfloat16)
    within = jnp.einsum("khij,kjhp->kihp", mixing, x_blocks, preferred_element_type=jnp.float32)
    weight = jnp.exp(cumulative[..., BLOCK - 1 :] - cumulative) * step_blocks
    x_float = x_blocks.astype(jnp.float32)
    weighted = (x_float * jnp.swapaxes(weight, 1, 2)[..., None]).astype(jnp.bfloat16)
    block_state = jnp.einsum(
        "kjhp,kjn->khpn", weighted, input_map, preferred_element_type=jnp.float32
    )
    block_decay = jnp.exp(cumulative[..., BLOCK - 1])

    def advance(carry, item):
        running, product = carry
        block_stop_index, state_here = item
        return (
            (block_stop_index[:, None, None] * running + state_here, product * block_stop_index),
            (running, product),
        )

    empty_state = jnp.zeros((heads_dev, HEAD_DIM, STATE), jnp.float32)
    (dev_state, dev_decay), (local_starts, prefixes) = lax.scan(
        advance, (empty_state, jnp.ones((heads_dev,), jnp.float32)), (block_decay, block_state)
    )
    def level(decay, state, axis):
        peers = lax.axis_size(axis)
        place = lax.axis_index(axis)
        packed = jnp.concatenate(
            [state, jnp.broadcast_to(decay[:, None, None], (heads_dev, 1, STATE))], axis=1
        ).astype(jnp.bfloat16)
        got = lax.all_to_all(
            jnp.broadcast_to(packed[None], (peers,) + packed.shape), axis, 0, 0, tiled=True
        ).astype(jnp.float32)
        tot_decay = jnp.ones_like(decay)
        tot_state = jnp.zeros_like(state)
        ex_decay = jnp.ones_like(decay)
        ex_state = jnp.zeros_like(state)
        for k in reversed(range(peers)):
            got_state = got[k, :, :HEAD_DIM]
            got_decay = got[k, :, HEAD_DIM, 0]
            earlier = k < place
            ex_state = jnp.where(earlier, ex_decay[:, None, None] * got_state + ex_state, ex_state)
            ex_decay = jnp.where(earlier, got_decay * ex_decay, ex_decay)
            tot_state = tot_decay[:, None, None] * got_state + tot_state
            tot_decay = got_decay * tot_decay
        return ex_decay, ex_state, tot_decay, tot_state

    in_decay, in_state, row_decay, row_state = level(dev_decay, dev_state, "x")
    mid_decay, mid_state, part_decay, part_state = level(row_decay, row_state, "zl")
    top_decay, top_state, _, _ = level(part_decay, part_state, "zh")
    before_state = mid_decay[:, None, None] * top_state + mid_state
    in_state = in_decay[:, None, None] * before_state + in_state
    incoming = in_state
    starting = local_starts + prefixes[:, :, None, None] * incoming[None]
    carried = jnp.einsum(
        "kin,khpn->kihp",
        output_map,
        starting.astype(jnp.bfloat16),
        preferred_element_type=jnp.float32,
    )
    carried = carried * jnp.swapaxes(jnp.exp(cumulative), 1, 2)[..., None]
    result_heads = within + carried + skip_weight[None, None, :, None] * x_float
    result_heads = result_heads.reshape(length, inner_dev)
    gated = result_heads * jax.nn.silu(gate_raw.astype(jnp.float32))
    scaled = jnp.concatenate(
        [(gated * norm_gain[None, :]).astype(jnp.bfloat16), (gated * gated).astype(jnp.bfloat16)], axis=1
    )
    width = out_weight.shape[1]
    extended = jnp.concatenate(
        [
            jnp.concatenate([out_weight, jnp.zeros((inner_dev, 128), out_weight.dtype)], axis=1),
            jnp.concatenate(
                [jnp.zeros((inner_dev, width), out_weight.dtype), jnp.ones((inner_dev, 128), out_weight.dtype)],
                axis=1,
            ),
        ],
        axis=0,
    )
    groups_here = lax.axis_size("tg")
    per = length // tp_size
    scaled = scaled.reshape((groups_here, 2, 2, per, 2 * inner_dev))
    scaled = jnp.transpose(scaled, (2, 1, 0, 3, 4))
    partial = jnp.einsum("...c,cn->...n", scaled, extended, preferred_element_type=jnp.float32)
    for axis in ("tc", "yl"):
        mine = lax.axis_index(axis)
        keep = lax.dynamic_index_in_dim(partial, mine, 0, keepdims=False)
        give = lax.dynamic_index_in_dim(partial, 1 - mine, 0, keepdims=False)
        partial = keep + lax.ppermute(give.astype(jnp.bfloat16), axis, [(0, 1), (1, 0)]).astype(jnp.float32)
    inverse = lax.rsqrt(partial[..., width] / (HEADS * HEAD_DIM // GROUPS) + 1e-05)
    held = (partial[..., :width] * inverse[..., None]).astype(jnp.bfloat16)
    arrived = lax.all_to_all(held, "tg", 0, 0, tiled=True)
    mixed = jnp.sum(arrived.astype(jnp.float32), axis=0)
    return mixed.astype(jnp.bfloat16)


TP_AXES = ("tg", "yl", "tc")


def solution(mesh):
    ctx_size = mesh.shape["ctx"]
    tp_size = mesh.shape["tp"]
    x_size = 4 if ctx_size % 4 == 0 else ctx_size
    z_size = ctx_size // x_size
    zl_size = 4 if z_size % 4 == 0 else z_size
    fine = Mesh(
        mesh.devices.reshape(z_size // zl_size, zl_size, x_size, tp_size // 4, 2, 2),
        ("zh", "zl", "x") + TP_AXES,
    )
    rows = ("zh", "zl", "x") + TP_AXES
    tp = TP_AXES
    placed = (
        P(rows, None),
        P(None, None, tp),
        P(None, tp),
        P(tp, None, None),
        P(None, tp),
        P(tp),
        P(),
        P(),
        P(tp),
        P(tp),
        P(tp),
        P(tp),
        P(tp, None),
    )
    return jax.shard_map(body, mesh=fine, in_specs=placed, out_specs=P(rows, None), check_vma=False)
```

```python
import jax
import jax.numpy as jnp
from jax import lax
from jax.sharding import Mesh, PartitionSpec as P

HEADS = 64
HEAD_DIM = 64
STATE = 128
GROUPS = 4
BLOCK = 256
KERNEL = 4


def shifted(x, axis, by):
    peers = lax.axis_size(axis)
    pairs = [(i, i + by) for i in range(peers) if 0 <= i + by < peers]
    return lax.ppermute(x, axis, pairs)


def swapped(x, axis, bit):
    peers = lax.axis_size(axis)
    return lax.ppermute(x, axis, [(i, i ^ bit) for i in range(peers)])


def gather_rows(rows, axis, bits):
    place = lax.axis_index(axis)
    peers = lax.axis_size(axis)
    held = rows
    for bit in reversed(bits):
        other = swapped(held, axis, bit)
        low = (place & bit) == 0
        held = jnp.where(low, jnp.stack([held, other]), jnp.stack([other, held]))
    return held


def halve(held, axis, bits):
    place = lax.axis_index(axis)
    for bit in bits:
        mine = (place // bit) % 2
        keep = lax.dynamic_index_in_dim(held, mine, 0, keepdims=False)
        give = lax.dynamic_index_in_dim(held, 1 - mine, 0, keepdims=False)
        held = keep + swapped(give.astype(jnp.bfloat16), axis, bit).astype(jnp.float32)
    return held


def causal_conv(prior_rows, raw_rows, conv_weight, conv_bias):
    joined = jnp.concatenate([prior_rows, raw_rows], axis=0).astype(jnp.float32)
    length = raw_rows.shape[0]
    running = jnp.broadcast_to(conv_bias[None, :], raw_rows.shape)
    for offset in range(conv_weight.shape[0]):
        running = running + conv_weight[offset][None, :] * joined[offset : offset + length]
    return jax.nn.silu(running).astype(jnp.bfloat16)


def body(
    hidden,
    in_weight,
    step_weight,
    group_weight,
    conv_inner,
    inner_bias,
    conv_group,
    group_bias,
    step_bias,
    log_rate,
    skip_weight,
    norm_gain,
    out_weight,
):
    tp_size = lax.axis_size(TP_AXES)
    heads_dev = log_rate.shape[0]
    inner_dev = in_weight.shape[2]
    group_cols = 2 * STATE
    per_group_dev = (HEADS // GROUPS) // heads_dev
    group_index = lax.axis_index("tg")
    zx_weight = in_weight.reshape(in_weight.shape[0], 2 * inner_dev)
    ring = ("tg", "yl")
    ring_size = lax.axis_size(ring)
    length = tp_size * hidden.shape[0]
    ring_rows = lax.all_to_all(
        jnp.broadcast_to(hidden[None], (ring_size,) + hidden.shape), ring, 0, 0, tiled=True
    )
    other_rows = lax.ppermute(ring_rows, "tc", [(0, 1), (1, 0)])
    first = lax.axis_index("tc") == 0
    stacked = jnp.where(
        first, jnp.stack([ring_rows, other_rows], axis=1), jnp.stack([other_rows, ring_rows], axis=1)
    ).reshape((length,) + hidden.shape[1:])

    def in_order(rows):
        return rows

    map_cols = jnp.transpose(group_weight, (2, 1, 0)).reshape(group_weight.shape[2], -1)
    joined = jnp.concatenate([zx_weight, step_weight, map_cols], axis=1)
    projected = in_order(
        jnp.einsum("...d,dn->...n", stacked, joined, preferred_element_type=jnp.float32)
    ).astype(jnp.bfloat16)
    gate_raw = projected[:, :inner_dev]
    inner_raw = projected[:, inner_dev : 2 * inner_dev]
    step_raw = projected[:, 2 * inner_dev : 2 * inner_dev + heads_dev]
    own_maps = projected[:, 2 * inner_dev + heads_dev :].reshape(length, GROUPS, -1)
    own_maps = jnp.moveaxis(own_maps, 1, 0)
    own_maps = jnp.broadcast_to(own_maps[:, None], (GROUPS, per_group_dev) + own_maps.shape[1:])
    own_maps = own_maps.reshape((tp_size,) + own_maps.shape[2:])
    got_maps = lax.all_to_all(own_maps, TP_AXES, 0, 0, tiled=True)
    map_part = jnp.transpose(got_maps, (1, 0, 2)).reshape(length, group_cols)
    border_rows = KERNEL - 1
    prior = shifted(
        jnp.concatenate([inner_raw[length - border_rows :], map_part[length - border_rows :]], axis=1),
        ("z", "x"),
        1,
    )
    inner_prior = prior[:, :inner_dev]
    map_prior = prior[:, inner_dev:]
    x_conv = causal_conv(inner_prior, inner_raw, conv_inner, inner_bias)
    own_taps = lax.dynamic_slice_in_dim(conv_group, group_index * group_cols, group_cols, 1)
    own_bias = lax.dynamic_slice_in_dim(group_bias, group_index * group_cols, group_cols, 0)
    maps = causal_conv(map_prior, map_part, own_taps, own_bias)
    step_size = jax.nn.softplus(step_raw.astype(jnp.float32) + step_bias[None, :])
    decay_rate = -jnp.exp(log_rate)
    blocks = length // BLOCK
    x_blocks = x_conv.reshape(blocks, BLOCK, heads_dev, HEAD_DIM)
    input_map = maps[:, :STATE].reshape(blocks, BLOCK, STATE)
    output_map = maps[:, STATE:].reshape(blocks, BLOCK, STATE)
    step_blocks = jnp.swapaxes(step_size.reshape(blocks, BLOCK, heads_dev), 1, 2)
    cumulative = jnp.cumsum(step_blocks * decay_rate[None, :, None], axis=2)
    scores = jnp.einsum("kin,kjn->kij", output_map, input_map, preferred_element_type=jnp.float32)
    causal = jnp.arange(BLOCK)[:, None] >= jnp.arange(BLOCK)[None, :]
    exponent = jnp.where(causal, cumulative[..., :, None] - cumulative[..., None, :], -jnp.inf)
    mixing = (scores[:, None] * jnp.exp(exponent) * step_blocks[..., None, :]).astype(jnp.bfloat16)
    within = jnp.einsum("khij,kjhp->kihp", mixing, x_blocks, preferred_element_type=jnp.float32)
    weight = jnp.exp(cumulative[..., BLOCK - 1 :] - cumulative) * step_blocks
    x_float = x_blocks.astype(jnp.float32)
    weighted = (x_float * jnp.swapaxes(weight, 1, 2)[..., None]).astype(jnp.bfloat16)
    block_state = jnp.einsum(
        "kjhp,kjn->khpn", weighted, input_map, preferred_element_type=jnp.float32
    )
    block_decay = jnp.exp(cumulative[..., BLOCK - 1])

    def advance(carry, item):
        running, product = carry
        block_stop_index, state_here = item
        return (
            (block_stop_index[:, None, None] * running + state_here, product * block_stop_index),
            (running, product),
        )

    empty_state = jnp.zeros((heads_dev, HEAD_DIM, STATE), jnp.float32)
    (dev_state, dev_decay), (local_starts, prefixes) = lax.scan(
        advance, (empty_state, jnp.ones((heads_dev,), jnp.float32)), (block_decay, block_state)
    )
    x_peers = lax.axis_size("x")
    x_place = lax.axis_index("x")
    packed = jnp.concatenate(
        [dev_state, jnp.broadcast_to(dev_decay[:, None, None], (heads_dev, 1, STATE))], axis=1
    ).astype(jnp.bfloat16)
    row = lax.all_to_all(
        jnp.broadcast_to(packed[None], (x_peers,) + packed.shape), "x", 0, 0, tiled=True
    ).astype(jnp.float32)
    row_decay = jnp.ones_like(dev_decay)
    row_state = jnp.zeros_like(dev_state)
    in_decay = jnp.ones_like(dev_decay)
    in_state = jnp.zeros_like(dev_state)
    for k in reversed(range(x_peers)):
        got_state = row[k, :, :HEAD_DIM]
        got_decay = row[k, :, HEAD_DIM, 0]
        earlier = k < x_place
        in_state = jnp.where(earlier, in_decay[:, None, None] * got_state + in_state, in_state)
        in_decay = jnp.where(earlier, got_decay * in_decay, in_decay)
        row_state = row_decay[:, None, None] * got_state + row_state
        row_decay = got_decay * row_decay
    z_peers = lax.axis_size("z")
    z_place = lax.axis_index("z")
    pre_decay = jnp.ones_like(dev_decay)
    pre_state = jnp.zeros_like(dev_state)
    run_decay = row_decay
    run_state = row_state
    reach = 1
    while reach < z_peers:
        packed = jnp.concatenate(
            [run_state, jnp.broadcast_to(run_decay[:, None, None], (heads_dev, 1, STATE))], axis=1
        )
        got = shifted(packed.astype(jnp.bfloat16), "z", reach).astype(jnp.float32)
        valid = z_place >= reach
        got_state = jnp.where(valid, got[:, :HEAD_DIM], 0.0)
        got_decay = jnp.where(valid, got[:, HEAD_DIM, 0], 1.0)
        pre_state = pre_decay[:, None, None] * got_state + pre_state
        pre_decay = got_decay * pre_decay
        run_state = run_decay[:, None, None] * got_state + run_state
        run_decay = got_decay * run_decay
        reach *= 2
    in_state = in_decay[:, None, None] * pre_state + in_state
    incoming = in_state
    starting = local_starts + prefixes[:, :, None, None] * incoming[None]
    carried = jnp.einsum(
        "kin,khpn->kihp",
        output_map,
        starting.astype(jnp.bfloat16),
        preferred_element_type=jnp.float32,
    )
    carried = carried * jnp.swapaxes(jnp.exp(cumulative), 1, 2)[..., None]
    result_heads = within + carried + skip_weight[None, None, :, None] * x_float
    result_heads = result_heads.reshape(length, inner_dev)
    gated = result_heads * jax.nn.silu(gate_raw.astype(jnp.float32))
    scaled = jnp.concatenate(
        [(gated * norm_gain[None, :]).astype(jnp.bfloat16), (gated * gated).astype(jnp.bfloat16)], axis=1
    )
    width = out_weight.shape[1]
    extended = jnp.concatenate(
        [
            jnp.concatenate([out_weight, jnp.zeros((inner_dev, 128), out_weight.dtype)], axis=1),
            jnp.concatenate(
                [jnp.zeros((inner_dev, width), out_weight.dtype), jnp.ones((inner_dev, 128), out_weight.dtype)],
                axis=1,
            ),
        ],
        axis=0,
    )
    groups_here = lax.axis_size("tg")
    per = length // tp_size
    scaled = scaled.reshape((groups_here, 2, 2, per, 2 * inner_dev))
    scaled = jnp.transpose(scaled, (2, 0, 1, 3, 4))
    partial = jnp.einsum("...c,cn->...n", scaled, extended, preferred_element_type=jnp.float32)
    mine = lax.axis_index("tc")
    keep = lax.dynamic_index_in_dim(partial, mine, 0, keepdims=False)
    give = lax.dynamic_index_in_dim(partial, 1 - mine, 0, keepdims=False)
    partial = keep + lax.ppermute(give.astype(jnp.bfloat16), "tc", [(0, 1), (1, 0)]).astype(jnp.float32)
    partial = partial.reshape((ring_size,) + partial.shape[2:])
    arrived = lax.all_to_all(partial.astype(jnp.bfloat16), ring, 0, 0, tiled=True)
    arrived = arrived.astype(jnp.float32).reshape((groups_here, ring_size // groups_here) + arrived.shape[1:])
    per_group = jnp.sum(arrived, axis=1)
    inverse = lax.rsqrt(per_group[..., width] / (HEADS * HEAD_DIM // GROUPS) + 1e-05)
    mixed = jnp.sum(per_group[..., :width] * inverse[..., None], axis=0)
    return mixed.astype(jnp.bfloat16)


TP_AXES = ("tg", "yl", "tc")


def solution(mesh):
    ctx_size = mesh.shape["ctx"]
    tp_size = mesh.shape["tp"]
    x_size = 4 if ctx_size % 4 == 0 else ctx_size
    fine = Mesh(
        mesh.devices.reshape(ctx_size // x_size, x_size, tp_size // 4, 2, 2), ("z", "x") + TP_AXES
    )
    rows = ("z", "x") + TP_AXES
    tp = TP_AXES
    placed = (
        P(rows, None),
        P(None, None, tp),
        P(None, tp),
        P(tp, None, None),
        P(None, tp),
        P(tp),
        P(),
        P(),
        P(tp),
        P(tp),
        P(tp),
        P(tp),
        P(tp, None),
    )
    return jax.shard_map(body, mesh=fine, in_specs=placed, out_specs=P(rows, None), check_vma=False)
```

```python
import jax
import jax.numpy as jnp
from jax import lax
from jax.sharding import Mesh, PartitionSpec as P

HEADS = 64
HEAD_DIM = 64
STATE = 128
GROUPS = 4
BLOCK = 256
KERNEL = 4


def shifted(x, axis, by):
    peers = lax.axis_size(axis)
    pairs = [(i, i + by) for i in range(peers) if 0 <= i + by < peers]
    return lax.ppermute(x, axis, pairs)


def swapped(x, axis, bit):
    peers = lax.axis_size(axis)
    return lax.ppermute(x, axis, [(i, i ^ bit) for i in range(peers)])


def gather_rows(rows, axis, bits):
    place = lax.axis_index(axis)
    peers = lax.axis_size(axis)
    held = rows
    for bit in reversed(bits):
        other = swapped(held, axis, bit)
        low = (place & bit) == 0
        held = jnp.where(low, jnp.stack([held, other]), jnp.stack([other, held]))
    return held


def halve(held, axis, bits):
    place = lax.axis_index(axis)
    for bit in bits:
        mine = (place // bit) % 2
        keep = lax.dynamic_index_in_dim(held, mine, 0, keepdims=False)
        give = lax.dynamic_index_in_dim(held, 1 - mine, 0, keepdims=False)
        held = keep + swapped(give.astype(jnp.bfloat16), axis, bit).astype(jnp.float32)
    return held


def causal_conv(prior_rows, raw_rows, conv_weight, conv_bias):
    joined = jnp.concatenate([prior_rows, raw_rows], axis=0).astype(jnp.float32)
    length = raw_rows.shape[0]
    running = jnp.broadcast_to(conv_bias[None, :], raw_rows.shape)
    for offset in range(conv_weight.shape[0]):
        running = running + conv_weight[offset][None, :] * joined[offset : offset + length]
    return jax.nn.silu(running).astype(jnp.bfloat16)


def body(
    hidden,
    in_weight,
    step_weight,
    group_weight,
    conv_inner,
    inner_bias,
    conv_group,
    group_bias,
    step_bias,
    log_rate,
    skip_weight,
    norm_gain,
    out_weight,
):
    tp_size = lax.axis_size(TP_AXES)
    heads_dev = log_rate.shape[0]
    inner_dev = in_weight.shape[2]
    group_cols = 2 * STATE
    per_group_dev = (HEADS // GROUPS) // heads_dev
    group_index = lax.axis_index("tg")
    zx_weight = in_weight.reshape(in_weight.shape[0], 2 * inner_dev)
    ring = ("tg", "yl")
    ring_size = lax.axis_size(ring)
    length = tp_size * hidden.shape[0]
    ring_rows = lax.all_to_all(
        jnp.broadcast_to(hidden[None], (ring_size,) + hidden.shape), ring, 0, 0, tiled=True
    )
    other_rows = lax.ppermute(ring_rows, "tc", [(0, 1), (1, 0)])
    first = lax.axis_index("tc") == 0
    stacked = jnp.where(
        first, jnp.stack([ring_rows, other_rows], axis=1), jnp.stack([other_rows, ring_rows], axis=1)
    ).reshape((length,) + hidden.shape[1:])

    def in_order(rows):
        return rows

    map_cols = jnp.transpose(group_weight, (2, 1, 0)).reshape(group_weight.shape[2], -1)
    joined = jnp.concatenate([zx_weight, step_weight, map_cols], axis=1)
    projected = in_order(
        jnp.einsum("...d,dn->...n", stacked, joined, preferred_element_type=jnp.float32)
    ).astype(jnp.bfloat16)
    gate_raw = projected[:, :inner_dev]
    inner_raw = projected[:, inner_dev : 2 * inner_dev]
    step_raw = projected[:, 2 * inner_dev : 2 * inner_dev + heads_dev]
    own_maps = projected[:, 2 * inner_dev + heads_dev :].reshape(length, GROUPS, -1)
    own_maps = jnp.moveaxis(own_maps, 1, 0)
    partner_maps = lax.ppermute(own_maps, "tc", [(0, 1), (1, 0)])
    chip_maps = jnp.where(
        first, jnp.stack([own_maps, partner_maps], axis=2), jnp.stack([partner_maps, own_maps], axis=2)
    ).reshape(own_maps.shape[:2] + (-1,))
    chip_maps = jnp.broadcast_to(
        chip_maps[:, None], (GROUPS, ring_size // GROUPS) + chip_maps.shape[1:]
    ).reshape((ring_size,) + chip_maps.shape[1:])
    got_maps = lax.all_to_all(chip_maps, ring, 0, 0, tiled=True)
    map_part = jnp.transpose(got_maps, (1, 0, 2)).reshape(length, group_cols)
    border_rows = KERNEL - 1
    prior = shifted(
        jnp.concatenate([inner_raw[length - border_rows :], map_part[length - border_rows :]], axis=1),
        ("z", "x"),
        1,
    )
    inner_prior = prior[:, :inner_dev]
    map_prior = prior[:, inner_dev:]
    x_conv = causal_conv(inner_prior, inner_raw, conv_inner, inner_bias)
    own_taps = lax.dynamic_slice_in_dim(conv_group, group_index * group_cols, group_cols, 1)
    own_bias = lax.dynamic_slice_in_dim(group_bias, group_index * group_cols, group_cols, 0)
    maps = causal_conv(map_prior, map_part, own_taps, own_bias)
    step_size = jax.nn.softplus(step_raw.astype(jnp.float32) + step_bias[None, :])
    decay_rate = -jnp.exp(log_rate)
    blocks = length // BLOCK
    x_blocks = x_conv.reshape(blocks, BLOCK, heads_dev, HEAD_DIM)
    input_map = maps[:, :STATE].reshape(blocks, BLOCK, STATE)
    output_map = maps[:, STATE:].reshape(blocks, BLOCK, STATE)
    step_blocks = jnp.swapaxes(step_size.reshape(blocks, BLOCK, heads_dev), 1, 2)
    cumulative = jnp.cumsum(step_blocks * decay_rate[None, :, None], axis=2)
    scores = jnp.einsum("kin,kjn->kij", output_map, input_map, preferred_element_type=jnp.float32)
    causal = jnp.arange(BLOCK)[:, None] >= jnp.arange(BLOCK)[None, :]
    exponent = jnp.where(causal, cumulative[..., :, None] - cumulative[..., None, :], -jnp.inf)
    mixing = (scores[:, None] * jnp.exp(exponent) * step_blocks[..., None, :]).astype(jnp.bfloat16)
    within = jnp.einsum("khij,kjhp->kihp", mixing, x_blocks, preferred_element_type=jnp.float32)
    weight = jnp.exp(cumulative[..., BLOCK - 1 :] - cumulative) * step_blocks
    x_float = x_blocks.astype(jnp.float32)
    weighted = (x_float * jnp.swapaxes(weight, 1, 2)[..., None]).astype(jnp.bfloat16)
    block_state = jnp.einsum(
        "kjhp,kjn->khpn", weighted, input_map, preferred_element_type=jnp.float32
    )
    block_decay = jnp.exp(cumulative[..., BLOCK - 1])

    def advance(carry, item):
        running, product = carry
        block_stop_index, state_here = item
        return (
            (block_stop_index[:, None, None] * running + state_here, product * block_stop_index),
            (running, product),
        )

    empty_state = jnp.zeros((heads_dev, HEAD_DIM, STATE), jnp.float32)
    (dev_state, dev_decay), (local_starts, prefixes) = lax.scan(
        advance, (empty_state, jnp.ones((heads_dev,), jnp.float32)), (block_decay, block_state)
    )
    x_peers = lax.axis_size("x")
    x_place = lax.axis_index("x")
    packed = jnp.concatenate(
        [dev_state, jnp.broadcast_to(dev_decay[:, None, None], (heads_dev, 1, STATE))], axis=1
    ).astype(jnp.bfloat16)
    row = lax.all_to_all(
        jnp.broadcast_to(packed[None], (x_peers,) + packed.shape), "x", 0, 0, tiled=True
    ).astype(jnp.float32)
    row_decay = jnp.ones_like(dev_decay)
    row_state = jnp.zeros_like(dev_state)
    in_decay = jnp.ones_like(dev_decay)
    in_state = jnp.zeros_like(dev_state)
    for k in reversed(range(x_peers)):
        got_state = row[k, :, :HEAD_DIM]
        got_decay = row[k, :, HEAD_DIM, 0]
        earlier = k < x_place
        in_state = jnp.where(earlier, in_decay[:, None, None] * got_state + in_state, in_state)
        in_decay = jnp.where(earlier, got_decay * in_decay, in_decay)
        row_state = row_decay[:, None, None] * got_state + row_state
        row_decay = got_decay * row_decay
    z_peers = lax.axis_size("z")
    z_place = lax.axis_index("z")
    pre_decay = jnp.ones_like(dev_decay)
    pre_state = jnp.zeros_like(dev_state)
    run_decay = row_decay
    run_state = row_state
    reach = 1
    while reach < z_peers:
        packed = jnp.concatenate(
            [run_state, jnp.broadcast_to(run_decay[:, None, None], (heads_dev, 1, STATE))], axis=1
        )
        got = shifted(packed.astype(jnp.bfloat16), "z", reach).astype(jnp.float32)
        valid = z_place >= reach
        got_state = jnp.where(valid, got[:, :HEAD_DIM], 0.0)
        got_decay = jnp.where(valid, got[:, HEAD_DIM, 0], 1.0)
        pre_state = pre_decay[:, None, None] * got_state + pre_state
        pre_decay = got_decay * pre_decay
        run_state = run_decay[:, None, None] * got_state + run_state
        run_decay = got_decay * run_decay
        reach *= 2
    in_state = in_decay[:, None, None] * pre_state + in_state
    incoming = in_state
    starting = local_starts + prefixes[:, :, None, None] * incoming[None]
    carried = jnp.einsum(
        "kin,khpn->kihp",
        output_map,
        starting.astype(jnp.bfloat16),
        preferred_element_type=jnp.float32,
    )
    carried = carried * jnp.swapaxes(jnp.exp(cumulative), 1, 2)[..., None]
    result_heads = within + carried + skip_weight[None, None, :, None] * x_float
    result_heads = result_heads.reshape(length, inner_dev)
    gated = result_heads * jax.nn.silu(gate_raw.astype(jnp.float32))
    scaled = jnp.concatenate(
        [(gated * norm_gain[None, :]).astype(jnp.bfloat16), (gated * gated).astype(jnp.bfloat16)], axis=1
    )
    width = out_weight.shape[1]
    extended = jnp.concatenate(
        [
            jnp.concatenate([out_weight, jnp.zeros((inner_dev, 128), out_weight.dtype)], axis=1),
            jnp.concatenate(
                [jnp.zeros((inner_dev, width), out_weight.dtype), jnp.ones((inner_dev, 128), out_weight.dtype)],
                axis=1,
            ),
        ],
        axis=0,
    )
    groups_here = lax.axis_size("tg")
    per = length // tp_size
    scaled = scaled.reshape((groups_here, 2, 2, per, 2 * inner_dev))
    scaled = jnp.transpose(scaled, (2, 0, 1, 3, 4))
    partial = jnp.einsum("...c,cn->...n", scaled, extended, preferred_element_type=jnp.float32)
    mine = lax.axis_index("tc")
    keep = lax.dynamic_index_in_dim(partial, mine, 0, keepdims=False)
    give = lax.dynamic_index_in_dim(partial, 1 - mine, 0, keepdims=False)
    partial = keep + lax.ppermute(give.astype(jnp.bfloat16), "tc", [(0, 1), (1, 0)]).astype(jnp.float32)
    partial = partial.reshape((ring_size,) + partial.shape[2:])
    arrived = lax.all_to_all(partial.astype(jnp.bfloat16), ring, 0, 0, tiled=True)
    arrived = arrived.astype(jnp.float32).reshape((groups_here, ring_size // groups_here) + arrived.shape[1:])
    per_group = jnp.sum(arrived, axis=1)
    inverse = lax.rsqrt(per_group[..., width] / (HEADS * HEAD_DIM // GROUPS) + 1e-05)
    mixed = jnp.sum(per_group[..., :width] * inverse[..., None], axis=0)
    return mixed.astype(jnp.bfloat16)


TP_AXES = ("tg", "yl", "tc")


def solution(mesh):
    ctx_size = mesh.shape["ctx"]
    tp_size = mesh.shape["tp"]
    x_size = 4 if ctx_size % 4 == 0 else ctx_size
    fine = Mesh(
        mesh.devices.reshape(ctx_size // x_size, x_size, tp_size // 4, 2, 2), ("z", "x") + TP_AXES
    )
    rows = ("z", "x") + TP_AXES
    tp = TP_AXES
    placed = (
        P(rows, None),
        P(None, None, tp),
        P(None, tp),
        P(tp, None, None),
        P(None, tp),
        P(tp),
        P(),
        P(),
        P(tp),
        P(tp),
        P(tp),
        P(tp),
        P(tp, None),
    )
    return jax.shard_map(body, mesh=fine, in_specs=placed, out_specs=P(rows, None), check_vma=False)
```

```python
import jax
import jax.numpy as jnp
from jax import lax
from jax.sharding import Mesh, PartitionSpec as P

HEADS = 64
HEAD_DIM = 64
STATE = 128
GROUPS = 4
BLOCK = 256
KERNEL = 4


def shifted(x, axis, by):
    peers = lax.axis_size(axis)
    pairs = [(i, i + by) for i in range(peers) if 0 <= i + by < peers]
    return lax.ppermute(x, axis, pairs)


def swapped(x, axis, bit):
    peers = lax.axis_size(axis)
    return lax.ppermute(x, axis, [(i, i ^ bit) for i in range(peers)])


def gather_rows(rows, axis, bits):
    place = lax.axis_index(axis)
    peers = lax.axis_size(axis)
    held = rows
    for bit in reversed(bits):
        other = swapped(held, axis, bit)
        low = (place & bit) == 0
        held = jnp.where(low, jnp.stack([held, other]), jnp.stack([other, held]))
    return held


def halve(held, axis, bits):
    place = lax.axis_index(axis)
    for bit in bits:
        mine = (place // bit) % 2
        keep = lax.dynamic_index_in_dim(held, mine, 0, keepdims=False)
        give = lax.dynamic_index_in_dim(held, 1 - mine, 0, keepdims=False)
        held = keep + swapped(give.astype(jnp.bfloat16), axis, bit).astype(jnp.float32)
    return held


def causal_conv(prior_rows, raw_rows, conv_weight, conv_bias):
    joined = jnp.concatenate([prior_rows, raw_rows], axis=0).astype(jnp.float32)
    length = raw_rows.shape[0]
    running = jnp.broadcast_to(conv_bias[None, :], raw_rows.shape)
    for offset in range(conv_weight.shape[0]):
        running = running + conv_weight[offset][None, :] * joined[offset : offset + length]
    return jax.nn.silu(running).astype(jnp.bfloat16)


def body(
    hidden,
    in_weight,
    step_weight,
    group_weight,
    conv_inner,
    inner_bias,
    conv_group,
    group_bias,
    step_bias,
    log_rate,
    skip_weight,
    norm_gain,
    out_weight,
):
    tp_size = lax.axis_size(TP_AXES)
    heads_dev = log_rate.shape[0]
    inner_dev = in_weight.shape[2]
    group_cols = 2 * STATE
    per_group_dev = (HEADS // GROUPS) // heads_dev
    group_index = lax.axis_index("tg")
    zx_weight = in_weight.reshape(in_weight.shape[0], 2 * inner_dev)
    ring = ("tg", "yl")
    ring_size = lax.axis_size(ring)
    length = tp_size * hidden.shape[0]
    ring_rows = lax.all_to_all(
        jnp.broadcast_to(hidden[None], (ring_size,) + hidden.shape), ring, 0, 0, tiled=True
    )
    other_rows = lax.ppermute(ring_rows, "tc", [(0, 1), (1, 0)])
    first = lax.axis_index("tc") == 0

    map_cols = jnp.transpose(group_weight, (2, 1, 0)).reshape(group_weight.shape[2], -1)
    joined = jnp.concatenate([zx_weight, step_weight, map_cols], axis=1)
    own_proj = jnp.einsum("...d,dn->...n", ring_rows, joined, preferred_element_type=jnp.float32)
    other_proj = jnp.einsum("...d,dn->...n", other_rows, joined, preferred_element_type=jnp.float32)
    projected = jnp.where(
        first, jnp.stack([own_proj, other_proj], axis=1), jnp.stack([other_proj, own_proj], axis=1)
    ).reshape((length, joined.shape[1])).astype(jnp.bfloat16)
    gate_raw = projected[:, :inner_dev]
    inner_raw = projected[:, inner_dev : 2 * inner_dev]
    step_raw = projected[:, 2 * inner_dev : 2 * inner_dev + heads_dev]
    own_maps = projected[:, 2 * inner_dev + heads_dev :].reshape(length, GROUPS, -1)
    own_maps = jnp.moveaxis(own_maps, 1, 0)
    own_maps = jnp.broadcast_to(own_maps[:, None], (GROUPS, per_group_dev) + own_maps.shape[1:])
    own_maps = own_maps.reshape((tp_size,) + own_maps.shape[2:])
    got_maps = lax.all_to_all(own_maps, TP_AXES, 0, 0, tiled=True)
    map_part = jnp.transpose(got_maps, (1, 0, 2)).reshape(length, group_cols)
    border_rows = KERNEL - 1
    prior = shifted(
        jnp.concatenate([inner_raw[length - border_rows :], map_part[length - border_rows :]], axis=1),
        ("z", "x"),
        1,
    )
    inner_prior = prior[:, :inner_dev]
    map_prior = prior[:, inner_dev:]
    x_conv = causal_conv(inner_prior, inner_raw, conv_inner, inner_bias)
    own_taps = lax.dynamic_slice_in_dim(conv_group, group_index * group_cols, group_cols, 1)
    own_bias = lax.dynamic_slice_in_dim(group_bias, group_index * group_cols, group_cols, 0)
    maps = causal_conv(map_prior, map_part, own_taps, own_bias)
    step_size = jax.nn.softplus(step_raw.astype(jnp.float32) + step_bias[None, :])
    decay_rate = -jnp.exp(log_rate)
    blocks = length // BLOCK
    x_blocks = x_conv.reshape(blocks, BLOCK, heads_dev, HEAD_DIM)
    input_map = maps[:, :STATE].reshape(blocks, BLOCK, STATE)
    output_map = maps[:, STATE:].reshape(blocks, BLOCK, STATE)
    step_blocks = jnp.swapaxes(step_size.reshape(blocks, BLOCK, heads_dev), 1, 2)
    cumulative = jnp.cumsum(step_blocks * decay_rate[None, :, None], axis=2)
    scores = jnp.einsum("kin,kjn->kij", output_map, input_map, preferred_element_type=jnp.float32)
    causal = jnp.arange(BLOCK)[:, None] >= jnp.arange(BLOCK)[None, :]
    exponent = jnp.where(causal, cumulative[..., :, None] - cumulative[..., None, :], -jnp.inf)
    mixing = (scores[:, None] * jnp.exp(exponent) * step_blocks[..., None, :]).astype(jnp.bfloat16)
    within = jnp.einsum("khij,kjhp->kihp", mixing, x_blocks, preferred_element_type=jnp.float32)
    weight = jnp.exp(cumulative[..., BLOCK - 1 :] - cumulative) * step_blocks
    x_float = x_blocks.astype(jnp.float32)
    weighted = (x_float * jnp.swapaxes(weight, 1, 2)[..., None]).astype(jnp.bfloat16)
    block_state = jnp.einsum(
        "kjhp,kjn->khpn", weighted, input_map, preferred_element_type=jnp.float32
    )
    block_decay = jnp.exp(cumulative[..., BLOCK - 1])

    def advance(carry, item):
        running, product = carry
        block_stop_index, state_here = item
        return (
            (block_stop_index[:, None, None] * running + state_here, product * block_stop_index),
            (running, product),
        )

    empty_state = jnp.zeros((heads_dev, HEAD_DIM, STATE), jnp.float32)
    (dev_state, dev_decay), (local_starts, prefixes) = lax.scan(
        advance, (empty_state, jnp.ones((heads_dev,), jnp.float32)), (block_decay, block_state)
    )
    x_peers = lax.axis_size("x")
    x_place = lax.axis_index("x")
    packed = jnp.concatenate(
        [dev_state, jnp.broadcast_to(dev_decay[:, None, None], (heads_dev, 1, STATE))], axis=1
    ).astype(jnp.bfloat16)
    row = lax.all_to_all(
        jnp.broadcast_to(packed[None], (x_peers,) + packed.shape), "x", 0, 0, tiled=True
    ).astype(jnp.float32)
    row_decay = jnp.ones_like(dev_decay)
    row_state = jnp.zeros_like(dev_state)
    in_decay = jnp.ones_like(dev_decay)
    in_state = jnp.zeros_like(dev_state)
    for k in reversed(range(x_peers)):
        got_state = row[k, :, :HEAD_DIM]
        got_decay = row[k, :, HEAD_DIM, 0]
        earlier = k < x_place
        in_state = jnp.where(earlier, in_decay[:, None, None] * got_state + in_state, in_state)
        in_decay = jnp.where(earlier, got_decay * in_decay, in_decay)
        row_state = row_decay[:, None, None] * got_state + row_state
        row_decay = got_decay * row_decay
    z_peers = lax.axis_size("z")
    z_place = lax.axis_index("z")
    pre_decay = jnp.ones_like(dev_decay)
    pre_state = jnp.zeros_like(dev_state)
    run_decay = row_decay
    run_state = row_state
    reach = 1
    while reach < z_peers:
        packed = jnp.concatenate(
            [run_state, jnp.broadcast_to(run_decay[:, None, None], (heads_dev, 1, STATE))], axis=1
        )
        got = shifted(packed.astype(jnp.bfloat16), "z", reach).astype(jnp.float32)
        valid = z_place >= reach
        got_state = jnp.where(valid, got[:, :HEAD_DIM], 0.0)
        got_decay = jnp.where(valid, got[:, HEAD_DIM, 0], 1.0)
        pre_state = pre_decay[:, None, None] * got_state + pre_state
        pre_decay = got_decay * pre_decay
        run_state = run_decay[:, None, None] * got_state + run_state
        run_decay = got_decay * run_decay
        reach *= 2
    in_state = in_decay[:, None, None] * pre_state + in_state
    incoming = in_state
    starting = local_starts + prefixes[:, :, None, None] * incoming[None]
    carried = jnp.einsum(
        "kin,khpn->kihp",
        output_map,
        starting.astype(jnp.bfloat16),
        preferred_element_type=jnp.float32,
    )
    carried = carried * jnp.swapaxes(jnp.exp(cumulative), 1, 2)[..., None]
    result_heads = within + carried + skip_weight[None, None, :, None] * x_float
    result_heads = result_heads.reshape(length, inner_dev)
    gated = result_heads * jax.nn.silu(gate_raw.astype(jnp.float32))
    scaled = jnp.concatenate(
        [(gated * norm_gain[None, :]).astype(jnp.bfloat16), (gated * gated).astype(jnp.bfloat16)], axis=1
    )
    width = out_weight.shape[1]
    extended = jnp.concatenate(
        [
            jnp.concatenate([out_weight, jnp.zeros((inner_dev, 128), out_weight.dtype)], axis=1),
            jnp.concatenate(
                [jnp.zeros((inner_dev, width), out_weight.dtype), jnp.ones((inner_dev, 128), out_weight.dtype)],
                axis=1,
            ),
        ],
        axis=0,
    )
    groups_here = lax.axis_size("tg")
    per = length // tp_size
    scaled = scaled.reshape((groups_here, 2, 2, per, 2 * inner_dev))
    scaled = jnp.transpose(scaled, (2, 0, 1, 3, 4))
    partial = jnp.einsum("...c,cn->...n", scaled, extended, preferred_element_type=jnp.float32)
    mine = lax.axis_index("tc")
    keep = lax.dynamic_index_in_dim(partial, mine, 0, keepdims=False)
    give = lax.dynamic_index_in_dim(partial, 1 - mine, 0, keepdims=False)
    partial = keep + lax.ppermute(give.astype(jnp.bfloat16), "tc", [(0, 1), (1, 0)]).astype(jnp.float32)
    partial = partial.reshape((ring_size,) + partial.shape[2:])
    arrived = lax.all_to_all(partial.astype(jnp.bfloat16), ring, 0, 0, tiled=True)
    arrived = arrived.astype(jnp.float32).reshape((groups_here, ring_size // groups_here) + arrived.shape[1:])
    per_group = jnp.sum(arrived, axis=1)
    inverse = lax.rsqrt(per_group[..., width] / (HEADS * HEAD_DIM // GROUPS) + 1e-05)
    mixed = jnp.sum(per_group[..., :width] * inverse[..., None], axis=0)
    return mixed.astype(jnp.bfloat16)


TP_AXES = ("tg", "yl", "tc")


def solution(mesh):
    ctx_size = mesh.shape["ctx"]
    tp_size = mesh.shape["tp"]
    x_size = 4 if ctx_size % 4 == 0 else ctx_size
    fine = Mesh(
        mesh.devices.reshape(ctx_size // x_size, x_size, tp_size // 4, 2, 2), ("z", "x") + TP_AXES
    )
    rows = ("z", "x") + TP_AXES
    tp = TP_AXES
    placed = (
        P(rows, None),
        P(None, None, tp),
        P(None, tp),
        P(tp, None, None),
        P(None, tp),
        P(tp),
        P(),
        P(),
        P(tp),
        P(tp),
        P(tp),
        P(tp),
        P(tp, None),
    )
    return jax.shard_map(body, mesh=fine, in_specs=placed, out_specs=P(rows, None), check_vma=False)
```
